32 devices in a mesh: rows: 4 (over y, x), cols: 8 (over z, core).
Axes of the slice: x: 2, y: 2, z: 4, core: 2. Of those that a mesh axis runs over, the one named last changes fastest.
Arguments:
- direct: float32 [49152, 1536], P(('rows', 'cols')), may hold values from -6 to 6
- adjoint: float32 [49152, 1536], P(('rows', 'cols')), may hold values from -6 to 6
- probes: float32 [1536, 256], replicated, may hold values from -6 to 6
Outputs:
- direct_modes: float32 [49152, 256], P(('rows', 'cols'))
- adjoint_modes: float32 [49152, 256], P(('rows', 'cols'))
The draws below stay inside these ranges and needn't reach their ends.
All inputs are finite; a program needn't handle non-finite values.
Results may differ from the reference program's by a relative error of at most 0.00013.
Values sent between devices are 32-bit elements; how exact they have to be, the bound alone decides.
No kernel may reach another device: no remote copies, remote signals or barrier semaphores. Data moves between devices by JAX's collectives and lax.ppermute only.
A program may use at most 128 MiB of HBM per device.

```python
import math
import jax
import jax.numpy as jnp
from jax import lax

SNAPS = 1536
PROBES = 256
NSTATE = 49152


def levels(own_key, shape, split, least, high):
    def one(axis_at, parts):
        heights = jax.random.uniform(jax.random.fold_in(jax.random.fold_in(own_key, 6), axis_at), (parts,), jnp.float32, least / len(split), high / len(split))
        return jnp.repeat(jnp.exp(heights), shape[axis_at] // parts).reshape((-1,) + (1,) * (len(shape) - axis_at - 1))

    gain = one(*split[0])
    for cut in split[1:]:
        gain = gain * one(*cut)
    return gain


def gaussian(stream_key, extent, width, most, pieces=(), held_as=jnp.bfloat16):
    gain = levels(stream_key, extent, pieces, -0.22, 0.18) if pieces else 1.0
    array = jax.random.normal(stream_key, extent, jnp.float32) * width * gain
    return jnp.minimum(jnp.maximum(array, -most), most).astype(held_as)


def setup_inputs(seed: int = 0) -> dict:
    keys = jax.random.split(jax.random.key(seed), 4)
    direct = gaussian(keys[0], (NSTATE, SNAPS), 1.0, 6.0, ((0, 32),), jnp.float32)
    adjoint = gaussian(keys[1], (NSTATE, SNAPS), 1.0, 6.0, ((0, 32),), jnp.float32)
    probes = gaussian(keys[2], (SNAPS, PROBES), 1.0, 6.0, (), jnp.float32)
    return dict(direct=direct, adjoint=adjoint, probes=probes)


def reference(direct, adjoint, probes):
    high = lax.Precision.HIGHEST
    scale = 1.0 / math.sqrt(NSTATE * SNAPS)
    hankel = jnp.dot(adjoint.T, direct, precision=high, preferred_element_type=jnp.float32) * scale
    coef_d = probes
    coef_a = probes
    for rnd in range(2):
        coef_a = jnp.dot(hankel, coef_d, precision=high, preferred_element_type=jnp.float32)
        coef_d = jnp.dot(hankel.T, coef_a, precision=high, preferred_element_type=jnp.float32)
    norm_factor = 1.0 / math.sqrt(SNAPS)
    direct_modes = jnp.dot(direct, coef_d, precision=high, preferred_element_type=jnp.float32) * norm_factor
    adjoint_modes = jnp.dot(adjoint, coef_a, precision=high, preferred_element_type=jnp.float32) * norm_factor
    return (direct_modes, adjoint_modes)
```

```python
import math

import jax
import jax.numpy as jnp
from jax import lax
from jax.sharding import PartitionSpec as P


def doubling_sum(x, axis):
    count = lax.axis_size(axis)
    step = 1
    while step < count:
        x = x + lax.ppermute(x, axis, [(i, i ^ step) for i in range(count)])
        step *= 2
    return x


def shards(direct, adjoint, probes):
    high = lax.Precision.HIGHEST
    fast = lax.Precision.HIGH
    row_count = lax.axis_size("rows")
    col_count = lax.axis_size("cols")
    state_rows, snap_count = direct.shape
    tile_rows = snap_count // row_count
    tile_cols = snap_count // col_count
    scale = 1.0 / math.sqrt(state_rows * row_count * col_count * snap_count)
    norm_factor = 1.0 / math.sqrt(snap_count)
    ordered = jnp.einsum(
        "nri,ncj->rcij",
        adjoint.reshape(state_rows, row_count, tile_rows),
        direct.reshape(state_rows, col_count, tile_cols),
        precision=fast,
        preferred_element_type=jnp.float32,
    ) * scale
    ordered = ordered.reshape(row_count * col_count * tile_rows, tile_cols)
    tile = lax.psum_scatter(ordered, ("rows", "cols"), scatter_dimension=0, tiled=True)
    col_index = lax.axis_index("cols")
    coef_d = lax.dynamic_slice_in_dim(probes, col_index * tile_cols, tile_cols, 0)
    coef_a = jnp.zeros((tile_rows, probes.shape[1]), jnp.float32)
    for rnd in range(2):
        coef_a = doubling_sum(
            jnp.dot(tile, coef_d, precision=high, preferred_element_type=jnp.float32), "cols"
        )
        coef_d = doubling_sum(
            jnp.dot(tile.T, coef_a, precision=high, preferred_element_type=jnp.float32), "rows"
        )
    direct_sum = jnp.dot(
        direct,
        lax.all_gather(coef_d, "cols", axis=0, tiled=True),
        precision=fast,
        preferred_element_type=jnp.float32,
    )
    adjoint_sum = jnp.dot(
        adjoint,
        lax.all_gather(coef_a, "rows", axis=0, tiled=True),
        precision=fast,
        preferred_element_type=jnp.float32,
    )
    return (direct_sum * norm_factor, adjoint_sum * norm_factor)


def solution(mesh):
    placed = (P(("rows", "cols"), None), P(("rows", "cols"), None), P())
    return jax.shard_map(
        shards,
        mesh=mesh,
        in_specs=placed,
        out_specs=(P(("rows", "cols"), None), P(("rows", "cols"), None)),
        check_vma=False,
    )
```

```python
import math

import jax
import jax.numpy as jnp
from jax import lax
from jax.sharding import PartitionSpec as P


def doubling_sum(x, axis, first, last):
    count = lax.axis_size(axis)
    step = first
    while step < last:
        x = x + lax.ppermute(x, axis, [(i, i ^ step) for i in range(count)])
        step *= 2
    return x


def shards(direct, adjoint, probes):
    high = lax.Precision.HIGHEST
    fast = lax.Precision.HIGH
    row_count = lax.axis_size("rows")
    col_count = lax.axis_size("cols")
    chip_count = col_count // 2
    state_rows, snap_count = direct.shape
    probe_half = probes.shape[1] // 2
    tile_rows = snap_count // row_count
    chip_cols = snap_count // chip_count
    scale = 1.0 / math.sqrt(state_rows * row_count * col_count * snap_count)
    norm_factor = 1.0 / math.sqrt(snap_count)
    partial_hankel = (
        jnp.dot(adjoint.T, direct, precision=fast, preferred_element_type=jnp.float32) * scale
    )
    strip = lax.psum_scatter(partial_hankel, "rows", scatter_dimension=0, tiled=True)
    tile = lax.psum_scatter(strip, "cols", scatter_dimension=1, tiled=True)
    col_index = lax.axis_index("cols")
    core = col_index % 2
    chip = col_index // 2
    other = lax.ppermute(tile, "cols", [(i, i ^ 1) for i in range(col_count)])
    first = core == 0
    chip_tile = jnp.concatenate(
        [jnp.where(first, tile, other), jnp.where(first, other, tile)], axis=1
    )
    own_probes = lax.dynamic_slice_in_dim(probes, core * probe_half, probe_half, 1)
    coef_d = lax.dynamic_slice_in_dim(own_probes, chip * chip_cols, chip_cols, 0)
    coef_a = jnp.zeros((tile_rows, probe_half), jnp.float32)
    for rnd in range(2):
        coef_a = doubling_sum(
            jnp.dot(chip_tile, coef_d, precision=high, preferred_element_type=jnp.float32),
            "cols", 2, col_count,
        )
        coef_d = doubling_sum(
            jnp.dot(chip_tile.T, coef_a, precision=high, preferred_element_type=jnp.float32),
            "rows", 1, row_count,
        )
    half_a = lax.all_gather(coef_a, "rows", axis=0, tiled=True)
    other_a = lax.ppermute(half_a, "cols", [(i, i ^ 1) for i in range(col_count)])
    full_a = jnp.concatenate(
        [jnp.where(first, half_a, other_a), jnp.where(first, other_a, half_a)], axis=1
    )
    gathered_d = lax.all_gather(coef_d, "cols", axis=0, tiled=False)
    full_d = (
        gathered_d.reshape(chip_count, 2, chip_cols, probe_half)
        .transpose(0, 2, 1, 3)
        .reshape(snap_count, 2 * probe_half)
    )
    direct_sum = jnp.dot(direct, full_d, precision=fast, preferred_element_type=jnp.float32)
    adjoint_sum = jnp.dot(adjoint, full_a, precision=fast, preferred_element_type=jnp.float32)
    return (direct_sum * norm_factor, adjoint_sum * norm_factor)


def solution(mesh):
    placed = (P(("rows", "cols"), None), P(("rows", "cols"), None), P())
    return jax.shard_map(
        shards,
        mesh=mesh,
        in_specs=placed,
        out_specs=(P(("rows", "cols"), None), P(("rows", "cols"), None)),
        check_vma=False,
    )
```

```python
import math

import jax
import jax.numpy as jnp
from jax import lax
from jax.sharding import PartitionSpec as P


def exchange(x, axis, step):
    count = lax.axis_size(axis)
    return lax.ppermute(x, axis, [(i, i ^ step) for i in range(count)])


def doubling_sum(x, axis, first, last):
    step = first
    while step < last:
        x = x + exchange(x, axis, step)
        step *= 2
    return x


def in_order(first, mine, theirs, axis):
    return jnp.concatenate(
        [jnp.where(first, mine, theirs), jnp.where(first, theirs, mine)], axis=axis
    )


def shards(direct, adjoint, probes):
    high = lax.Precision.HIGHEST
    fast = lax.Precision.HIGH
    row_count = lax.axis_size("rows")
    col_count = lax.axis_size("cols")
    chip_count = col_count // 2
    state_rows, snap_count = direct.shape
    probe_half = probes.shape[1] // 2
    half_rows = snap_count // 2
    part_rows = half_rows // row_count
    chip_cols = snap_count // chip_count
    scale = 1.0 / math.sqrt(state_rows * row_count * col_count * snap_count)
    norm_factor = 1.0 / math.sqrt(snap_count)
    col_index = lax.axis_index("cols")
    core = col_index % 2
    chip = col_index // 2
    first = core == 0
    partial_hankel = (
        jnp.dot(adjoint.T, direct, precision=fast, preferred_element_type=jnp.float32) * scale
    )
    keep = lax.dynamic_slice_in_dim(partial_hankel, core * half_rows, half_rows, 0)
    send = lax.dynamic_slice_in_dim(partial_hankel, (1 - core) * half_rows, half_rows, 0)
    chip_sum = keep + exchange(send, "cols", 1)
    strip = lax.psum_scatter(chip_sum, "rows", scatter_dimension=0, tiled=True)
    bits = chip_count.bit_length() - 1
    strip = strip.reshape((part_rows,) + (2,) * bits + (chip_cols,))
    for bit in range(bits):
        mine = (chip >> bit) % 2
        kept = lax.dynamic_index_in_dim(strip, mine, axis=strip.ndim - 2, keepdims=False)
        sent = lax.dynamic_index_in_dim(strip, 1 - mine, axis=strip.ndim - 2, keepdims=False)
        strip = kept + exchange(sent, "cols", 2 << bit)
    tile = strip
    chip_tile = in_order(first, tile, exchange(tile, "cols", 1), 0)
    own_probes = lax.dynamic_slice_in_dim(probes, core * probe_half, probe_half, 1)
    coef_d = lax.dynamic_slice_in_dim(own_probes, chip * chip_cols, chip_cols, 0)
    coef_a = jnp.zeros((2 * part_rows, probe_half), jnp.float32)
    for rnd in range(2):
        coef_a = doubling_sum(
            jnp.dot(chip_tile, coef_d, precision=high, preferred_element_type=jnp.float32),
            "cols", 2, col_count,
        )
        coef_d = doubling_sum(
            jnp.dot(chip_tile.T, coef_a, precision=high, preferred_element_type=jnp.float32),
            "rows", 1, row_count,
        )
    gathered_a = lax.all_gather(coef_a, "rows", axis=0, tiled=False)
    half_a = (
        gathered_a.reshape(row_count, 2, part_rows, probe_half)
        .transpose(1, 0, 2, 3)
        .reshape(snap_count, probe_half)
    )
    full_a = in_order(first, half_a, exchange(half_a, "cols", 1), 1)
    gathered_d = lax.all_gather(coef_d, "cols", axis=0, tiled=False)
    full_d = (
        gathered_d.reshape(chip_count, 2, chip_cols, probe_half)
        .transpose(0, 2, 1, 3)
        .reshape(snap_count, 2 * probe_half)
    )
    direct_sum = jnp.dot(direct, full_d, precision=fast, preferred_element_type=jnp.float32)
    adjoint_sum = jnp.dot(adjoint, full_a, precision=fast, preferred_element_type=jnp.float32)
    return (direct_sum * norm_factor, adjoint_sum * norm_factor)


def solution(mesh):
    placed = (P(("rows", "cols"), None), P(("rows", "cols"), None), P())
    return jax.shard_map(
        shards,
        mesh=mesh,
        in_specs=placed,
        out_specs=(P(("rows", "cols"), None), P(("rows", "cols"), None)),
        check_vma=False,
    )
```

```python
import math

import jax
import jax.numpy as jnp
from jax import lax
from jax.sharding import PartitionSpec as P


def exchange(x, axis, step):
    count = lax.axis_size(axis)
    return lax.ppermute(x, axis, [(i, i ^ step) for i in range(count)])


def doubling_sum(x, axis, first, last):
    step = first
    while step < last:
        x = x + exchange(x, axis, step)
        step *= 2
    return x


def in_order(first, mine, theirs, axis):
    return jnp.concatenate(
        [jnp.where(first, mine, theirs), jnp.where(first, theirs, mine)], axis=axis
    )


def shards(direct, adjoint, probes):
    high = lax.Precision.HIGHEST
    fast = lax.Precision.HIGH
    row_count = lax.axis_size("rows")
    col_count = lax.axis_size("cols")
    chip_count = col_count // 2
    state_rows, snap_count = direct.shape
    probe_half = probes.shape[1] // 2
    half_rows = snap_count // 2
    part_rows = half_rows // row_count
    chip_cols = snap_count // chip_count
    scale = 1.0 / math.sqrt(state_rows * row_count * col_count * snap_count)
    norm_factor = 1.0 / math.sqrt(snap_count)
    col_index = lax.axis_index("cols")
    core = col_index % 2
    chip = col_index // 2
    first = core == 0
    def partial_rows(start):
        columns = lax.dynamic_slice_in_dim(adjoint, start, half_rows, 1)
        return jnp.dot(columns.T, direct, precision=fast, preferred_element_type=jnp.float32) * scale

    received = exchange(partial_rows((1 - core) * half_rows), "cols", 1)
    kept_rows = lax.optimization_barrier(partial_rows(core * half_rows))
    chip_sum = kept_rows + received
    strip = lax.psum_scatter(chip_sum, "rows", scatter_dimension=0, tiled=True)
    bits = chip_count.bit_length() - 1
    strip = strip.reshape((part_rows,) + (2,) * bits + (chip_cols,))
    for bit in range(bits):
        mine = (chip >> bit) % 2
        kept = lax.dynamic_index_in_dim(strip, mine, axis=strip.ndim - 2, keepdims=False)
        sent = lax.dynamic_index_in_dim(strip, 1 - mine, axis=strip.ndim - 2, keepdims=False)
        strip = kept + exchange(sent, "cols", 2 << bit)
    tile = strip
    chip_tile = in_order(first, tile, exchange(tile, "cols", 1), 0)
    own_probes = lax.dynamic_slice_in_dim(probes, core * probe_half, probe_half, 1)
    coef_d = lax.dynamic_slice_in_dim(own_probes, chip * chip_cols, chip_cols, 0)
    coef_a = jnp.zeros((2 * part_rows, probe_half), jnp.float32)
    for rnd in range(2):
        coef_a = doubling_sum(
            jnp.dot(chip_tile, coef_d, precision=high, preferred_element_type=jnp.float32),
            "cols", 2, col_count,
        )
        coef_d = doubling_sum(
            jnp.dot(chip_tile.T, coef_a, precision=high, preferred_element_type=jnp.float32),
            "rows", 1, row_count,
        )
    gathered_a = lax.all_gather(coef_a, "rows", axis=0, tiled=False)
    half_a = (
        gathered_a.reshape(row_count, 2, part_rows, probe_half)
        .transpose(1, 0, 2, 3)
        .reshape(snap_count, probe_half)
    )
    full_a = in_order(first, half_a, exchange(half_a, "cols", 1), 1)
    gathered_d = lax.all_gather(coef_d, "cols", axis=0, tiled=False)
    full_d = (
        gathered_d.reshape(chip_count, 2, chip_cols, probe_half)
        .transpose(0, 2, 1, 3)
        .reshape(snap_count, 2 * probe_half)
    )
    direct_sum = jnp.dot(direct, full_d, precision=fast, preferred_element_type=jnp.float32)
    adjoint_sum = jnp.dot(adjoint, full_a, precision=fast, preferred_element_type=jnp.float32)
    return (direct_sum * norm_factor, adjoint_sum * norm_factor)


def solution(mesh):
    placed = (P(("rows", "cols"), None), P(("rows", "cols"), None), P())
    return jax.shard_map(
        shards,
        mesh=mesh,
        in_specs=placed,
        out_specs=(P(("rows", "cols"), None), P(("rows", "cols"), None)),
        check_vma=False,
    )
```

```python
import math

import jax
import jax.numpy as jnp
from jax import lax
from jax.sharding import PartitionSpec as P


def exchange(x, axis, step):
    count = lax.axis_size(axis)
    return lax.ppermute(x, axis, [(i, i ^ step) for i in range(count)])


def doubling_sum(x, axis, first, last):
    step = first
    while step < last:
        x = x + exchange(x, axis, step)
        step *= 2
    return x


def in_order(first, mine, theirs, axis):
    return jnp.concatenate(
        [jnp.where(first, mine, theirs), jnp.where(first, theirs, mine)], axis=axis
    )


def shards(direct, adjoint, probes):
    high = lax.Precision.HIGHEST
    fast = lax.Precision.HIGH
    row_count = lax.axis_size("rows")
    col_count = lax.axis_size("cols")
    chip_count = col_count // 2
    state_rows, snap_count = direct.shape
    probe_half = probes.shape[1] // 2
    half_rows = snap_count // 2
    part_rows = half_rows // row_count
    chip_cols = snap_count // chip_count
    scale = 1.0 / math.sqrt(state_rows * row_count * col_count * snap_count)
    norm_factor = 1.0 / math.sqrt(snap_count)
    col_index = lax.axis_index("cols")
    core = col_index % 2
    chip = col_index // 2
    first = core == 0
    def partial_rows(start):
        columns = lax.dynamic_slice_in_dim(adjoint, start, half_rows, 1)
        return jnp.dot(columns.T, direct, precision=fast, preferred_element_type=jnp.float32) * scale

    received = exchange(partial_rows((1 - core) * half_rows), "cols", 1)
    kept_rows = lax.optimization_barrier(partial_rows(core * half_rows))
    chip_sum = kept_rows + received
    strip = lax.psum_scatter(chip_sum, "rows", scatter_dimension=0, tiled=True)
    bits = chip_count.bit_length() - 1
    strip = strip.reshape((part_rows,) + (2,) * bits + (chip_cols,))
    for bit in range(bits):
        mine = (chip >> bit) % 2
        kept = lax.dynamic_index_in_dim(strip, mine, axis=strip.ndim - 2, keepdims=False)
        sent = lax.dynamic_index_in_dim(strip, 1 - mine, axis=strip.ndim - 2, keepdims=False)
        strip = kept + exchange(sent, "cols", 2 << bit)
    tile = strip
    chip_tile = in_order(first, tile, exchange(tile, "cols", 1), 0)
    own_probes = lax.dynamic_slice_in_dim(probes, core * probe_half, probe_half, 1)
    coef_d = lax.dynamic_slice_in_dim(own_probes, chip * chip_cols, chip_cols, 0)
    coef_a = jnp.zeros((2 * part_rows, probe_half), jnp.float32)
    for rnd in range(2):
        coef_a = doubling_sum(
            jnp.dot(chip_tile, coef_d, precision=high, preferred_element_type=jnp.float32),
            "cols", 2, col_count,
        )
        coef_d = doubling_sum(
            jnp.dot(chip_tile.T, coef_a, precision=high, preferred_element_type=jnp.float32),
            "rows", 1, row_count,
        )
    gathered_a = coef_a[None]
    step = 1
    while step < row_count:
        low = (lax.axis_index("rows") & step) == 0
        gathered_a = in_order(low, gathered_a, exchange(gathered_a, "rows", step), 0)
        step *= 2
    half_a = (
        gathered_a.reshape(row_count, 2, part_rows, probe_half)
        .transpose(1, 0, 2, 3)
        .reshape(snap_count, probe_half)
    )
    full_a = in_order(first, half_a, exchange(half_a, "cols", 1), 1)
    gathered_d = lax.all_gather(coef_d, "cols", axis=0, tiled=False)
    full_d = (
        gathered_d.reshape(chip_count, 2, chip_cols, probe_half)
        .transpose(0, 2, 1, 3)
        .reshape(snap_count, 2 * probe_half)
    )
    direct_sum = jnp.dot(direct, full_d, precision=fast, preferred_element_type=jnp.float32)
    adjoint_sum = jnp.dot(adjoint, full_a, precision=fast, preferred_element_type=jnp.float32)
    return (direct_sum * norm_factor, adjoint_sum * norm_factor)


def solution(mesh):
    placed = (P(("rows", "cols"), None), P(("rows", "cols"), None), P())
    return jax.shard_map(
        shards,
        mesh=mesh,
        in_specs=placed,
        out_specs=(P(("rows", "cols"), None), P(("rows", "cols"), None)),
        check_vma=False,
    )
```

```python
import math

import jax
import jax.numpy as jnp
from jax import lax
from jax.sharding import PartitionSpec as P


def exchange(x, axis, step):
    count = lax.axis_size(axis)
    return lax.ppermute(x, axis, [(i, i ^ step) for i in range(count)])


def doubling_sum(x, axis, first, last):
    step = first
    while step < last:
        x = x + exchange(x, axis, step)
        step *= 2
    return x


def in_order(first, mine, theirs, axis):
    return jnp.concatenate(
        [jnp.where(first, mine, theirs), jnp.where(first, theirs, mine)], axis=axis
    )


def shards(direct, adjoint, probes):
    high = lax.Precision.HIGHEST
    fast = lax.Precision.HIGH
    row_count = lax.axis_size("rows")
    col_count = lax.axis_size("cols")
    chip_count = col_count // 2
    state_rows, snap_count = direct.shape
    probe_half = probes.shape[1] // 2
    half_rows = snap_count // 2
    part_rows = half_rows // row_count
    chip_cols = snap_count // chip_count
    scale = 1.0 / math.sqrt(state_rows * row_count * col_count * snap_count)
    norm_factor = 1.0 / math.sqrt(snap_count)
    col_index = lax.axis_index("cols")
    core = col_index % 2
    chip = col_index // 2
    first = core == 0
    def partial_rows(start):
        columns = lax.dynamic_slice_in_dim(adjoint, start, half_rows, 1)
        return jnp.dot(columns.T, direct, precision=fast, preferred_element_type=jnp.float32) * scale

    received = exchange(partial_rows((1 - core) * half_rows), "cols", 1)
    kept_rows = lax.optimization_barrier(partial_rows(core * half_rows))
    chip_sum = kept_rows + received
    strip = lax.psum_scatter(chip_sum, "rows", scatter_dimension=0, tiled=True)
    bits = chip_count.bit_length() - 1
    strip = strip.reshape((part_rows,) + (2,) * bits + (chip_cols,))
    for bit in range(bits):
        mine = (chip >> bit) % 2
        kept = lax.dynamic_index_in_dim(strip, mine, axis=strip.ndim - 2, keepdims=False)
        sent = lax.dynamic_index_in_dim(strip, 1 - mine, axis=strip.ndim - 2, keepdims=False)
        strip = kept + exchange(sent, "cols", 2 << bit)
    tile = strip
    chip_tile = in_order(first, tile, exchange(tile, "cols", 1), 0)
    own_probes = lax.dynamic_slice_in_dim(probes, core * probe_half, probe_half, 1)
    probes_d = lax.dynamic_slice_in_dim(own_probes, chip * chip_cols, chip_cols, 0)
    chains_a, chains_d = [], []
    quarter = probe_half // 2
    for chain in range(2):
        coef_d = probes_d[:, chain * quarter:(chain + 1) * quarter]
        for rnd in range(2):
            coef_a = doubling_sum(
                jnp.dot(chip_tile, coef_d, precision=high, preferred_element_type=jnp.float32),
                "cols", 2, col_count,
            )
            coef_d = doubling_sum(
                jnp.dot(chip_tile.T, coef_a, precision=high, preferred_element_type=jnp.float32),
                "rows", 1, row_count,
            )
        chains_a.append(coef_a)
        chains_d.append(coef_d)
    coef_a = jnp.concatenate(chains_a, axis=1)
    coef_d = jnp.concatenate(chains_d, axis=1)
    gathered_a = lax.all_gather(coef_a, "rows", axis=0, tiled=False)
    half_a = (
        gathered_a.reshape(row_count, 2, part_rows, probe_half)
        .transpose(1, 0, 2, 3)
        .reshape(snap_count, probe_half)
    )
    full_a = in_order(first, half_a, exchange(half_a, "cols", 1), 1)
    gathered_d = lax.all_gather(coef_d, "cols", axis=0, tiled=False)
    full_d = (
        gathered_d.reshape(chip_count, 2, chip_cols, probe_half)
        .transpose(0, 2, 1, 3)
        .reshape(snap_count, 2 * probe_half)
    )
    direct_sum = jnp.dot(direct, full_d, precision=fast, preferred_element_type=jnp.float32)
    adjoint_sum = jnp.dot(adjoint, full_a, precision=fast, preferred_element_type=jnp.float32)
    return (direct_sum * norm_factor, adjoint_sum * norm_factor)


def solution(mesh):
    placed = (P(("rows", "cols"), None), P(("rows", "cols"), None), P())
    return jax.shard_map(
        shards,
        mesh=mesh,
        in_specs=placed,
        out_specs=(P(("rows", "cols"), None), P(("rows", "cols"), None)),
        check_vma=False,
    )
```

```python
import math

import jax
import jax.numpy as jnp
from jax import lax
from jax.sharding import PartitionSpec as P


def exchange(x, axis, step):
    count = lax.axis_size(axis)
    return lax.ppermute(x, axis, [(i, i ^ step) for i in range(count)])


def doubling_sum(x, axis, first, last):
    step = first
    while step < last:
        x = x + exchange(x, axis, step)
        step *= 2
    return x


def in_order(first, mine, theirs, axis):
    return jnp.concatenate(
        [jnp.where(first, mine, theirs), jnp.where(first, theirs, mine)], axis=axis
    )


def shards(direct, adjoint, probes):
    high = lax.Precision.HIGHEST
    fast = lax.Precision.HIGH
    row_count = lax.axis_size("rows")
    col_count = lax.axis_size("cols")
    chip_count = col_count // 2
    state_rows, snap_count = direct.shape
    probe_half = probes.shape[1] // 2
    half_rows = snap_count // 2
    part_rows = half_rows // row_count
    chip_cols = snap_count // chip_count
    scale = 1.0 / math.sqrt(state_rows * row_count * col_count * snap_count)
    norm_factor = 1.0 / math.sqrt(snap_count)
    col_index = lax.axis_index("cols")
    core = col_index % 2
    chip = col_index // 2
    first = core == 0
    def partial_rows(start):
        columns = lax.dynamic_slice_in_dim(adjoint, start, half_rows, 1)
        return jnp.dot(columns.T, direct, precision=fast, preferred_element_type=jnp.float32) * scale

    received = exchange(partial_rows((1 - core) * half_rows), "cols", 1)
    kept_rows = lax.optimization_barrier(partial_rows(core * half_rows))
    chip_sum = kept_rows + received
    strip = lax.psum_scatter(chip_sum, "rows", scatter_dimension=0, tiled=True)
    bits = chip_count.bit_length() - 1
    strip = strip.reshape((part_rows,) + (2,) * bits + (chip_cols,))
    for bit in range(bits):
        mine = (chip >> bit) % 2
        kept = lax.dynamic_index_in_dim(strip, mine, axis=strip.ndim - 2, keepdims=False)
        sent = lax.dynamic_index_in_dim(strip, 1 - mine, axis=strip.ndim - 2, keepdims=False)
        strip = kept + exchange(sent, "cols", 2 << bit)
    tile = strip
    chip_tile = in_order(first, tile, exchange(tile, "cols", 1), 0)
    own_probes = lax.dynamic_slice_in_dim(probes, core * probe_half, probe_half, 1)
    probes_d = lax.dynamic_slice_in_dim(own_probes, chip * chip_cols, chip_cols, 0)
    chains_a, chains_d = [], []
    quarter = probe_half // 2
    for chain in range(2):
        coef_d = probes_d[:, chain * quarter:(chain + 1) * quarter]
        for rnd in range(2):
            coef_a = doubling_sum(
                jnp.dot(chip_tile, coef_d, precision=high, preferred_element_type=jnp.float32),
                "cols", 2, col_count,
            )
            coef_d = doubling_sum(
                jnp.dot(chip_tile.T, coef_a, precision=high, preferred_element_type=jnp.float32),
                "rows", 1, row_count,
            )
        gathered = coef_a[None]
        step = 1
        while step < row_count:
            low = (lax.axis_index("rows") & step) == 0
            gathered = in_order(low, gathered, exchange(gathered, "rows", step), 0)
            step *= 2
        chains_a.append(gathered)
        chains_d.append(coef_d)
    gathered_a = jnp.concatenate(chains_a, axis=2)
    coef_d = jnp.concatenate(chains_d, axis=1)
    half_a = (
        gathered_a.reshape(row_count, 2, part_rows, probe_half)
        .transpose(1, 0, 2, 3)
        .reshape(snap_count, probe_half)
    )
    full_a = in_order(first, half_a, exchange(half_a, "cols", 1), 1)
    gathered_d = lax.all_gather(coef_d, "cols", axis=0, tiled=False)
    full_d = (
        gathered_d.reshape(chip_count, 2, chip_cols, probe_half)
        .transpose(0, 2, 1, 3)
        .reshape(snap_count, 2 * probe_half)
    )
    direct_sum = jnp.dot(direct, full_d, precision=fast, preferred_element_type=jnp.float32)
    adjoint_sum = jnp.dot(adjoint, full_a, precision=fast, preferred_element_type=jnp.float32)
    return (direct_sum * norm_factor, adjoint_sum * norm_factor)


def solution(mesh):
    placed = (P(("rows", "cols"), None), P(("rows", "cols"), None), P())
    return jax.shard_map(
        shards,
        mesh=mesh,
        in_specs=placed,
        out_specs=(P(("rows", "cols"), None), P(("rows", "cols"), None)),
        check_vma=False,
    )
```

```python
import math

import jax
import jax.numpy as jnp
from jax import lax
from jax.sharding import PartitionSpec as P


def exchange(x, axis, step):
    count = lax.axis_size(axis)
    return lax.ppermute(x, axis, [(i, i ^ step) for i in range(count)])


def doubling_sum(x, axis, first, last):
    step = first
    while step < last:
        x = x + exchange(x, axis, step)
        step *= 2
    return x


def in_order(first, mine, theirs, axis):
    return jnp.concatenate(
        [jnp.where(first, mine, theirs), jnp.where(first, theirs, mine)], axis=axis
    )


def shards(direct, adjoint, probes):
    high = lax.Precision.HIGHEST
    fast = lax.Precision.HIGH
    row_count = lax.axis_size("rows")
    col_count = lax.axis_size("cols")
    chip_count = col_count // 2
    state_rows, snap_count = direct.shape
    probe_half = probes.shape[1] // 2
    half_rows = snap_count // 2
    part_rows = half_rows // row_count
    chip_cols = snap_count // chip_count
    scale = 1.0 / math.sqrt(state_rows * row_count * col_count * snap_count)
    norm_factor = 1.0 / math.sqrt(snap_count)
    col_index = lax.axis_index("cols")
    core = col_index % 2
    chip = col_index // 2
    first = core == 0
    def partial_rows(start):
        columns = lax.dynamic_slice_in_dim(adjoint, start, half_rows, 1)
        return jnp.dot(columns.T, direct, precision=fast, preferred_element_type=jnp.float32) * scale

    received = exchange(partial_rows((1 - core) * half_rows), "cols", 1)
    kept_rows = lax.optimization_barrier(partial_rows(core * half_rows))
    chip_sum = kept_rows + received
    strip = lax.psum_scatter(chip_sum, "rows", scatter_dimension=0, tiled=True)
    bits = chip_count.bit_length() - 1
    strip = strip.reshape((part_rows,) + (2,) * bits + (chip_cols,))
    for bit in range(bits):
        mine = (chip >> bit) % 2
        kept = lax.dynamic_index_in_dim(strip, mine, axis=strip.ndim - 2, keepdims=False)
        sent = lax.dynamic_index_in_dim(strip, 1 - mine, axis=strip.ndim - 2, keepdims=False)
        strip = kept + exchange(sent, "cols", 2 << bit)
    tile = strip
    chip_tile = in_order(first, tile, exchange(tile, "cols", 1), 0)
    own_probes = lax.dynamic_slice_in_dim(probes, core * probe_half, probe_half, 1)
    probes_d = lax.dynamic_slice_in_dim(own_probes, chip * chip_cols, chip_cols, 0)
    chains_a, chains_d = [], []
    chain_count = 4
    quarter = probe_half // chain_count
    for chain in range(chain_count):
        coef_d = probes_d[:, chain * quarter:(chain + 1) * quarter]
        for rnd in range(2):
            coef_a = doubling_sum(
                jnp.dot(chip_tile, coef_d, precision=high, preferred_element_type=jnp.float32),
                "cols", 2, col_count,
            )
            coef_d = doubling_sum(
                jnp.dot(chip_tile.T, coef_a, precision=high, preferred_element_type=jnp.float32),
                "rows", 1, row_count,
            )
        gathered = coef_a[None]
        step = 1
        while step < row_count:
            low = (lax.axis_index("rows") & step) == 0
            gathered = in_order(low, gathered, exchange(gathered, "rows", step), 0)
            step *= 2
        chains_a.append(gathered)
        chains_d.append(coef_d)
    gathered_a = jnp.concatenate(chains_a, axis=2)
    coef_d = jnp.concatenate(chains_d, axis=1)
    half_a = (
        gathered_a.reshape(row_count, 2, part_rows, probe_half)
        .transpose(1, 0, 2, 3)
        .reshape(snap_count, probe_half)
    )
    full_a = in_order(first, half_a, exchange(half_a, "cols", 1), 1)
    gathered_d = lax.all_gather(coef_d, "cols", axis=0, tiled=False)
    full_d = (
        gathered_d.reshape(chip_count, 2, chip_cols, probe_half)
        .transpose(0, 2, 1, 3)
        .reshape(snap_count, 2 * probe_half)
    )
    direct_sum = jnp.dot(direct, full_d, precision=fast, preferred_element_type=jnp.float32)
    adjoint_sum = jnp.dot(adjoint, full_a, precision=fast, preferred_element_type=jnp.float32)
    return (direct_sum * norm_factor, adjoint_sum * norm_factor)


def solution(mesh):
    placed = (P(("rows", "cols"), None), P(("rows", "cols"), None), P())
    return jax.shard_map(
        shards,
        mesh=mesh,
        in_specs=placed,
        out_specs=(P(("rows", "cols"), None), P(("rows", "cols"), None)),
        check_vma=False,
    )
```

```python
import math

import jax
import jax.numpy as jnp
from jax import lax
from jax.sharding import PartitionSpec as P


def exchange(x, axis, step):
    count = lax.axis_size(axis)
    return lax.ppermute(x, axis, [(i, i ^ step) for i in range(count)])


def doubling_sum(x, axis, first, last):
    step = first
    while step < last:
        x = x + exchange(x, axis, step)
        step *= 2
    return x


def in_order(first, mine, theirs, axis):
    return jnp.concatenate(
        [jnp.where(first, mine, theirs), jnp.where(first, theirs, mine)], axis=axis
    )


def shards(direct, adjoint, probes):
    high = lax.Precision.HIGHEST
    fast = lax.Precision.HIGH
    row_count = lax.axis_size("rows")
    col_count = lax.axis_size("cols")
    chip_count = col_count // 2
    state_rows, snap_count = direct.shape
    probe_half = probes.shape[1] // 2
    half_rows = snap_count // 2
    part_rows = half_rows // row_count
    chip_cols = snap_count // chip_count
    scale = 1.0 / math.sqrt(state_rows * row_count * col_count * snap_count)
    norm_factor = 1.0 / math.sqrt(snap_count)
    col_index = lax.axis_index("cols")
    core = col_index % 2
    chip = col_index // 2
    first = core == 0
    def partial_rows(start):
        columns = lax.dynamic_slice_in_dim(adjoint, start, half_rows, 1)
        return jnp.dot(columns.T, direct, precision=fast, preferred_element_type=jnp.float32) * scale

    received = exchange(partial_rows((1 - core) * half_rows), "cols", 1)
    kept_rows = lax.optimization_barrier(partial_rows(core * half_rows))
    chip_sum = kept_rows + received
    row_bits = row_count.bit_length() - 1
    row_index = lax.axis_index("rows")
    chunk_cols = snap_count // row_bits
    chunks = []
    for rot in range(row_bits):
        part = chip_sum[:, rot * chunk_cols:(rot + 1) * chunk_cols]
        part = part.reshape((2,) * row_bits + (part_rows, chunk_cols))
        left = list(range(row_bits - 1, -1, -1))
        for k in range(row_bits):
            bit = (rot + k) % row_bits
            axis = left.index(bit)
            mine = (row_index >> bit) % 2
            kept = lax.dynamic_index_in_dim(part, mine, axis=axis, keepdims=False)
            sent = lax.dynamic_index_in_dim(part, 1 - mine, axis=axis, keepdims=False)
            part = kept + exchange(sent, "rows", 1 << bit)
            left.pop(axis)
        chunks.append(part)
    strip = jnp.concatenate(chunks, axis=1)
    bits = chip_count.bit_length() - 1
    strip = strip.reshape((part_rows,) + (2,) * bits + (chip_cols,))
    for bit in range(bits):
        mine = (chip >> bit) % 2
        kept = lax.dynamic_index_in_dim(strip, mine, axis=strip.ndim - 2, keepdims=False)
        sent = lax.dynamic_index_in_dim(strip, 1 - mine, axis=strip.ndim - 2, keepdims=False)
        strip = kept + exchange(sent, "cols", 2 << bit)
    tile = strip
    chip_tile = in_order(first, tile, exchange(tile, "cols", 1), 0)
    own_probes = lax.dynamic_slice_in_dim(probes, core * probe_half, probe_half, 1)
    probes_d = lax.dynamic_slice_in_dim(own_probes, chip * chip_cols, chip_cols, 0)
    chains_a, chains_d = [], []
    quarter = probe_half // 2
    for chain in range(2):
        coef_d = probes_d[:, chain * quarter:(chain + 1) * quarter]
        for rnd in range(2):
            coef_a = doubling_sum(
                jnp.dot(chip_tile, coef_d, precision=high, preferred_element_type=jnp.float32),
                "cols", 2, col_count,
            )
            coef_d = doubling_sum(
                jnp.dot(chip_tile.T, coef_a, precision=high, preferred_element_type=jnp.float32),
                "rows", 1, row_count,
            )
        chains_a.append(coef_a)
        chains_d.append(coef_d)
    coef_a = jnp.concatenate(chains_a, axis=1)
    coef_d = jnp.concatenate(chains_d, axis=1)
    gathered_a = lax.all_gather(coef_a, "rows", axis=0, tiled=False)
    half_a = (
        gathered_a.reshape(row_count, 2, part_rows, probe_half)
        .transpose(1, 0, 2, 3)
        .reshape(snap_count, probe_half)
    )
    full_a = in_order(first, half_a, exchange(half_a, "cols", 1), 1)
    col_bits = col_count.bit_length() - 1
    gathered_d = coef_d.reshape((1,) * col_bits + coef_d.shape)
    for bit in range(col_bits - 1, -1, -1):
        low = (col_index >> bit) % 2 == 0
        gathered_d = in_order(low, gathered_d, exchange(gathered_d, "cols", 1 << bit), col_bits - 1 - bit)
    full_d = (
        gathered_d.reshape(chip_count, 2, chip_cols, probe_half)
        .transpose(0, 2, 1, 3)
        .reshape(snap_count, 2 * probe_half)
    )
    direct_sum = jnp.dot(direct, full_d, precision=fast, preferred_element_type=jnp.float32)
    adjoint_sum = jnp.dot(adjoint, full_a, precision=fast, preferred_element_type=jnp.float32)
    return (direct_sum * norm_factor, adjoint_sum * norm_factor)


def solution(mesh):
    placed = (P(("rows", "cols"), None), P(("rows", "cols"), None), P())
    return jax.shard_map(
        shards,
        mesh=mesh,
        in_specs=placed,
        out_specs=(P(("rows", "cols"), None), P(("rows", "cols"), None)),
        check_vma=False,
    )
```

```python
import math

import jax
import jax.numpy as jnp
from jax import lax
from jax.sharding import PartitionSpec as P


def exchange(x, axis, step):
    count = lax.axis_size(axis)
    return lax.ppermute(x, axis, [(i, i ^ step) for i in range(count)])


def doubling_sum(x, axis, first, last):
    step = first
    while step < last:
        x = x + exchange(x, axis, step)
        step *= 2
    return x


def in_order(first, mine, theirs, axis):
    return jnp.concatenate(
        [jnp.where(first, mine, theirs), jnp.where(first, theirs, mine)], axis=axis
    )


def shards(direct, adjoint, probes):
    high = lax.Precision.HIGHEST
    fast = lax.Precision.HIGH
    row_count = lax.axis_size("rows")
    col_count = lax.axis_size("cols")
    chip_count = col_count // 2
    state_rows, snap_count = direct.shape
    probe_half = probes.shape[1] // 2
    half_rows = snap_count // 2
    part_rows = half_rows // row_count
    chip_cols = snap_count // chip_count
    scale = 1.0 / math.sqrt(state_rows * row_count * col_count * snap_count)
    norm_factor = 1.0 / math.sqrt(snap_count)
    col_index = lax.axis_index("cols")
    core = col_index % 2
    chip = col_index // 2
    first = core == 0
    def partial_rows(start):
        columns = lax.dynamic_slice_in_dim(adjoint, start, half_rows, 1)
        return jnp.dot(columns.T, direct, precision=fast, preferred_element_type=jnp.float32) * scale

    received = exchange(partial_rows((1 - core) * half_rows), "cols", 1)
    kept_rows = lax.optimization_barrier(partial_rows(core * half_rows))
    chip_sum = kept_rows + received
    row_bits = row_count.bit_length() - 1
    row_index = lax.axis_index("rows")
    chunk_cols = snap_count // row_bits
    chunks = []
    for rot in range(row_bits):
        part = chip_sum[:, rot * chunk_cols:(rot + 1) * chunk_cols]
        part = part.reshape((2,) * row_bits + (part_rows, chunk_cols))
        left = list(range(row_bits - 1, -1, -1))
        for k in range(row_bits):
            bit = (rot + k) % row_bits
            axis = left.index(bit)
            mine = (row_index >> bit) % 2
            kept = lax.dynamic_index_in_dim(part, mine, axis=axis, keepdims=False)
            sent = lax.dynamic_index_in_dim(part, 1 - mine, axis=axis, keepdims=False)
            part = kept + exchange(sent, "rows", 1 << bit)
            left.pop(axis)
        chunks.append(part)
    strip = jnp.concatenate(chunks, axis=1)
    bits = chip_count.bit_length() - 1
    strip = strip.reshape((part_rows,) + (2,) * bits + (chip_cols,))
    for bit in range(bits):
        mine = (chip >> bit) % 2
        kept = lax.dynamic_index_in_dim(strip, mine, axis=strip.ndim - 2, keepdims=False)
        sent = lax.dynamic_index_in_dim(strip, 1 - mine, axis=strip.ndim - 2, keepdims=False)
        strip = kept + exchange(sent, "cols", 2 << bit)
    tile = strip
    chip_tile = in_order(first, tile, exchange(tile, "cols", 1), 0)
    own_probes = lax.dynamic_slice_in_dim(probes, core * probe_half, probe_half, 1)
    probes_d = lax.dynamic_slice_in_dim(own_probes, chip * chip_cols, chip_cols, 0)
    chains_a, chains_d = [], []
    quarter = probe_half // 2
    for chain in range(2):
        coef_d = probes_d[:, chain * quarter:(chain + 1) * quarter]
        for rnd in range(2):
            coef_a = doubling_sum(
                jnp.dot(chip_tile, coef_d, precision=high, preferred_element_type=jnp.float32),
                "cols", 2, col_count,
            )
            coef_d = doubling_sum(
                jnp.dot(chip_tile.T, coef_a, precision=high, preferred_element_type=jnp.float32),
                "rows", 1, row_count,
            )
        gathered = coef_a[None]
        step = 1
        while step < row_count:
            low = (row_index & step) == 0
            gathered = in_order(low, gathered, exchange(gathered, "rows", step), 0)
            step *= 2
        chains_a.append(gathered)
        chains_d.append(coef_d)
    gathered_a = jnp.concatenate(chains_a, axis=2)
    coef_d = jnp.concatenate(chains_d, axis=1)
    half_a = (
        gathered_a.reshape(row_count, 2, part_rows, probe_half)
        .transpose(1, 0, 2, 3)
        .reshape(snap_count, probe_half)
    )
    full_a = in_order(first, half_a, exchange(half_a, "cols", 1), 1)
    col_bits = col_count.bit_length() - 1
    gathered_d = coef_d.reshape((1,) * col_bits + coef_d.shape)
    for bit in range(col_bits - 1, -1, -1):
        low = (col_index >> bit) % 2 == 0
        gathered_d = in_order(low, gathered_d, exchange(gathered_d, "cols", 1 << bit), col_bits - 1 - bit)
    full_d = (
        gathered_d.reshape(chip_count, 2, chip_cols, probe_half)
        .transpose(0, 2, 1, 3)
        .reshape(snap_count, 2 * probe_half)
    )
    direct_sum = jnp.dot(direct, full_d, precision=fast, preferred_element_type=jnp.float32)
    adjoint_sum = jnp.dot(adjoint, full_a, precision=fast, preferred_element_type=jnp.float32)
    return (direct_sum * norm_factor, adjoint_sum * norm_factor)


def solution(mesh):
    placed = (P(("rows", "cols"), None), P(("rows", "cols"), None), P())
    return jax.shard_map(
        shards,
        mesh=mesh,
        in_specs=placed,
        out_specs=(P(("rows", "cols"), None), P(("rows", "cols"), None)),
        check_vma=False,
    )
```

```python
import math

import jax
import jax.numpy as jnp
from jax import lax
from jax.sharding import PartitionSpec as P


def exchange(x, axis, step):
    count = lax.axis_size(axis)
    return lax.ppermute(x, axis, [(i, i ^ step) for i in range(count)])


def doubling_sum(x, axis, first, last):
    step = first
    while step < last:
        x = x + exchange(x, axis, step)
        step *= 2
    return x


def in_order(first, mine, theirs, axis):
    return jnp.concatenate(
        [jnp.where(first, mine, theirs), jnp.where(first, theirs, mine)], axis=axis
    )


def shards(direct, adjoint, probes):
    fast = lax.Precision.HIGH
    row_count = lax.axis_size("rows")
    col_count = lax.axis_size("cols")
    chip_count = col_count // 2
    state_rows, snap_count = direct.shape
    probe_half = probes.shape[1] // 2
    half_rows = snap_count // 2
    part_rows = half_rows // row_count
    chip_cols = snap_count // chip_count
    scale = 1.0 / math.sqrt(state_rows * row_count * col_count * snap_count)
    norm_factor = 1.0 / math.sqrt(snap_count)
    col_index = lax.axis_index("cols")
    core = col_index % 2
    chip = col_index // 2
    first = core == 0
    def partial_rows(start):
        columns = lax.dynamic_slice_in_dim(adjoint, start, half_rows, 1)
        return jnp.dot(columns.T, direct, precision=fast, preferred_element_type=jnp.float32) * scale

    received = exchange(partial_rows((1 - core) * half_rows), "cols", 1)
    kept_rows = lax.optimization_barrier(partial_rows(core * half_rows))
    chip_sum = kept_rows + received
    row_bits = row_count.bit_length() - 1
    row_index = lax.axis_index("rows")
    chunk_cols = snap_count // row_bits
    chunks = []
    for rot in range(row_bits):
        part = chip_sum[:, rot * chunk_cols:(rot + 1) * chunk_cols]
        part = part.reshape((2,) * row_bits + (part_rows, chunk_cols))
        left = list(range(row_bits - 1, -1, -1))
        for k in range(row_bits):
            bit = (rot + k) % row_bits
            axis = left.index(bit)
            mine = (row_index >> bit) % 2
            kept = lax.dynamic_index_in_dim(part, mine, axis=axis, keepdims=False)
            sent = lax.dynamic_index_in_dim(part, 1 - mine, axis=axis, keepdims=False)
            part = kept + exchange(sent, "rows", 1 << bit)
            left.pop(axis)
        chunks.append(part)
    strip = jnp.concatenate(chunks, axis=1)
    bits = chip_count.bit_length() - 1
    strip = strip.reshape((part_rows,) + (2,) * bits + (chip_cols,))
    for bit in range(bits):
        mine = (chip >> bit) % 2
        kept = lax.dynamic_index_in_dim(strip, mine, axis=strip.ndim - 2, keepdims=False)
        sent = lax.dynamic_index_in_dim(strip, 1 - mine, axis=strip.ndim - 2, keepdims=False)
        strip = kept + exchange(sent, "cols", 2 << bit)
    tile = strip
    chip_tile = in_order(first, tile, exchange(tile, "cols", 1), 0)
    own_probes = lax.dynamic_slice_in_dim(probes, core * probe_half, probe_half, 1)
    probes_d = lax.dynamic_slice_in_dim(own_probes, chip * chip_cols, chip_cols, 0)
    chains_a, chains_d = [], []
    quarter = probe_half // 2
    for chain in range(2):
        coef_d = probes_d[:, chain * quarter:(chain + 1) * quarter]
        for rnd in range(2):
            coef_a = doubling_sum(
                jnp.dot(chip_tile, coef_d, precision=fast, preferred_element_type=jnp.float32),
                "cols", 2, col_count,
            )
            coef_d = doubling_sum(
                jnp.dot(chip_tile.T, coef_a, precision=fast, preferred_element_type=jnp.float32),
                "rows", 1, row_count,
            )
        gathered = coef_a[None]
        step = 1
        while step < row_count:
            low = (row_index & step) == 0
            gathered = in_order(low, gathered, exchange(gathered, "rows", step), 0)
            step *= 2
        chains_a.append(gathered)
        chains_d.append(coef_d)
    gathered_a = jnp.concatenate(chains_a, axis=2)
    coef_d = jnp.concatenate(chains_d, axis=1)
    half_a = (
        gathered_a.reshape(row_count, 2, part_rows, probe_half)
        .transpose(1, 0, 2, 3)
        .reshape(snap_count, probe_half)
    )
    full_a = in_order(first, half_a, exchange(half_a, "cols", 1), 1)
    col_bits = col_count.bit_length() - 1
    gathered_d = coef_d.reshape((1,) * col_bits + coef_d.shape)
    for bit in range(col_bits - 1, -1, -1):
        low = (col_index >> bit) % 2 == 0
        gathered_d = in_order(low, gathered_d, exchange(gathered_d, "cols", 1 << bit), col_bits - 1 - bit)
    full_d = (
        gathered_d.reshape(chip_count, 2, chip_cols, probe_half)
        .transpose(0, 2, 1, 3)
        .reshape(snap_count, 2 * probe_half)
    )
    direct_sum = jnp.dot(direct, full_d, precision=fast, preferred_element_type=jnp.float32)
    adjoint_sum = jnp.dot(adjoint, full_a, precision=fast, preferred_element_type=jnp.float32)
    return (direct_sum * norm_factor, adjoint_sum * norm_factor)


def solution(mesh):
    placed = (P(("rows", "cols"), None), P(("rows", "cols"), None), P())
    return jax.shard_map(
        shards,
        mesh=mesh,
        in_specs=placed,
        out_specs=(P(("rows", "cols"), None), P(("rows", "cols"), None)),
        check_vma=False,
    )
```

```python
import math

import jax
import jax.numpy as jnp
from jax import lax
from jax.sharding import PartitionSpec as P


def exchange(x, axis, step):
    count = lax.axis_size(axis)
    return lax.ppermute(x, axis, [(i, i ^ step) for i in range(count)])


def doubling_sum(x, axis, first, last):
    step = first
    while step < last:
        x = x + exchange(x, axis, step)
        step *= 2
    return x


def in_order(first, mine, theirs, axis):
    return jnp.concatenate(
        [jnp.where(first, mine, theirs), jnp.where(first, theirs, mine)], axis=axis
    )


def shards(direct, adjoint, probes):
    high = lax.Precision.HIGHEST
    fast = lax.Precision.HIGH
    row_count = lax.axis_size("rows")
    col_count = lax.axis_size("cols")
    chip_count = col_count // 2
    state_rows, snap_count = direct.shape
    probe_half = probes.shape[1] // 2
    half_rows = snap_count // 2
    part_rows = half_rows // row_count
    chip_cols = snap_count // chip_count
    scale = 1.0 / math.sqrt(state_rows * row_count * col_count * snap_count)
    norm_factor = 1.0 / math.sqrt(snap_count)
    col_index = lax.axis_index("cols")
    core = col_index % 2
    chip = col_index // 2
    first = core == 0
    def partial_rows(start):
        columns = lax.dynamic_slice_in_dim(adjoint, start, half_rows, 1)
        return jnp.dot(columns.T, direct, precision=fast, preferred_element_type=jnp.float32) * scale

    received = exchange(partial_rows((1 - core) * half_rows), "cols", 1)
    kept_rows = lax.optimization_barrier(partial_rows(core * half_rows))
    chip_sum = kept_rows + received
    row_bits = row_count.bit_length() - 1
    row_index = lax.axis_index("rows")
    chunk_cols = snap_count // row_bits
    chunks = []
    for rot in range(row_bits):
        part = chip_sum[:, rot * chunk_cols:(rot + 1) * chunk_cols]
        part = part.reshape((2,) * row_bits + (part_rows, chunk_cols))
        left = list(range(row_bits - 1, -1, -1))
        for k in range(row_bits):
            bit = (rot + k) % row_bits
            axis = left.index(bit)
            mine = (row_index >> bit) % 2
            kept = lax.dynamic_index_in_dim(part, mine, axis=axis, keepdims=False)
            sent = lax.dynamic_index_in_dim(part, 1 - mine, axis=axis, keepdims=False)
            part = kept + exchange(sent, "rows", 1 << bit)
            left.pop(axis)
        chunks.append(part)
    strip = jnp.concatenate(chunks, axis=1)
    bits = chip_count.bit_length() - 1
    strip = strip.reshape((part_rows,) + (2,) * bits + (chip_cols,))
    for bit in range(bits):
        mine = (chip >> bit) % 2
        kept = lax.dynamic_index_in_dim(strip, mine, axis=strip.ndim - 2, keepdims=False)
        sent = lax.dynamic_index_in_dim(strip, 1 - mine, axis=strip.ndim - 2, keepdims=False)
        strip = kept + exchange(sent, "cols", 2 << bit)
    tile = strip
    chip_tile = in_order(first, tile, exchange(tile, "cols", 1), 0)
    own_probes = lax.dynamic_slice_in_dim(probes, core * probe_half, probe_half, 1)
    probes_d = lax.dynamic_slice_in_dim(own_probes, chip * chip_cols, chip_cols, 0)
    chains_a, chains_d = [], []
    col_bits = col_count.bit_length() - 1
    quarter = probe_half // 2
    for chain in range(2):
        coef_d = probes_d[:, chain * quarter:(chain + 1) * quarter]
        for rnd in range(2):
            coef_a = doubling_sum(
                jnp.dot(chip_tile, coef_d, precision=high, preferred_element_type=jnp.float32),
                "cols", 2, col_count,
            )
            coef_d = doubling_sum(
                jnp.dot(chip_tile.T, coef_a, precision=high, preferred_element_type=jnp.float32),
                "rows", 1, row_count,
            )
        gathered = coef_a[None]
        step = 1
        while step < row_count:
            low = (row_index & step) == 0
            gathered = in_order(low, gathered, exchange(gathered, "rows", step), 0)
            step *= 2
        chains_a.append(gathered)
        gathered = coef_d.reshape((1,) * col_bits + coef_d.shape)
        for bit in range(col_bits - 1, -1, -1):
            low = (col_index >> bit) % 2 == 0
            gathered = in_order(low, gathered, exchange(gathered, "cols", 1 << bit), col_bits - 1 - bit)
        chains_d.append(gathered)
    gathered_a = jnp.concatenate(chains_a, axis=2)
    gathered_d = jnp.concatenate(chains_d, axis=-1)
    half_a = (
        gathered_a.reshape(row_count, 2, part_rows, probe_half)
        .transpose(1, 0, 2, 3)
        .reshape(snap_count, probe_half)
    )
    full_a = in_order(first, half_a, exchange(half_a, "cols", 1), 1)
    full_d = (
        gathered_d.reshape(chip_count, 2, chip_cols, probe_half)
        .transpose(0, 2, 1, 3)
        .reshape(snap_count, 2 * probe_half)
    )
    direct_sum = jnp.dot(direct, full_d, precision=fast, preferred_element_type=jnp.float32)
    adjoint_sum = jnp.dot(adjoint, full_a, precision=fast, preferred_element_type=jnp.float32)
    return (direct_sum * norm_factor, adjoint_sum * norm_factor)


def solution(mesh):
    placed = (P(("rows", "cols"), None), P(("rows", "cols"), None), P())
    return jax.shard_map(
        shards,
        mesh=mesh,
        in_specs=placed,
        out_specs=(P(("rows", "cols"), None), P(("rows", "cols"), None)),
        check_vma=False,
    )
```

```python
import math

import jax
import jax.numpy as jnp
from jax import lax
from jax.sharding import PartitionSpec as P


def exchange(x, axis, step):
    count = lax.axis_size(axis)
    return lax.ppermute(x, axis, [(i, i ^ step) for i in range(count)])


def doubling_sum(x, axis, first, last):
    step = first
    while step < last:
        x = x + exchange(x, axis, step)
        step *= 2
    return x


def in_order(first, mine, theirs, axis):
    return jnp.concatenate(
        [jnp.where(first, mine, theirs), jnp.where(first, theirs, mine)], axis=axis
    )


def shards(direct, adjoint, probes):
    high = lax.Precision.HIGHEST
    fast = lax.Precision.HIGH
    row_count = lax.axis_size("rows")
    col_count = lax.axis_size("cols")
    chip_count = col_count // 2
    state_rows, snap_count = direct.shape
    probe_half = probes.shape[1] // 2
    half_rows = snap_count // 2
    part_rows = half_rows // row_count
    chip_cols = snap_count // chip_count
    scale = 1.0 / math.sqrt(state_rows * row_count * col_count * snap_count)
    norm_factor = 1.0 / math.sqrt(snap_count)
    col_index = lax.axis_index("cols")
    core = col_index % 2
    chip = col_index // 2
    first = core == 0
    def partial_rows(start):
        columns = lax.dynamic_slice_in_dim(adjoint, start, half_rows, 1)
        return jnp.dot(columns.T, direct, precision=fast, preferred_element_type=jnp.float32) * scale

    received = exchange(partial_rows((1 - core) * half_rows), "cols", 1)
    kept_rows = lax.optimization_barrier(partial_rows(core * half_rows))
    chip_sum = kept_rows + received
    row_bits = row_count.bit_length() - 1
    row_index = lax.axis_index("rows")
    chunk_cols = snap_count // row_bits
    chunks = []
    for rot in range(row_bits):
        part = chip_sum[:, rot * chunk_cols:(rot + 1) * chunk_cols]
        part = part.reshape((2,) * row_bits + (part_rows, chunk_cols))
        left = list(range(row_bits - 1, -1, -1))
        for k in range(row_bits):
            bit = (rot + k) % row_bits
            axis = left.index(bit)
            mine = (row_index >> bit) % 2
            kept = lax.dynamic_index_in_dim(part, mine, axis=axis, keepdims=False)
            sent = lax.dynamic_index_in_dim(part, 1 - mine, axis=axis, keepdims=False)
            part = kept + exchange(sent, "rows", 1 << bit)
            left.pop(axis)
        chunks.append(part)
    strip = jnp.concatenate(chunks, axis=1)
    bits = chip_count.bit_length() - 1
    strip = strip.reshape((part_rows,) + (2,) * bits + (chip_cols,))
    for bit in range(bits):
        mine = (chip >> bit) % 2
        kept = lax.dynamic_index_in_dim(strip, mine, axis=strip.ndim - 2, keepdims=False)
        sent = lax.dynamic_index_in_dim(strip, 1 - mine, axis=strip.ndim - 2, keepdims=False)
        strip = kept + exchange(sent, "cols", 2 << bit)
    tile = strip
    chip_tile = in_order(first, tile, exchange(tile, "cols", 1), 0)
    own_probes = lax.dynamic_slice_in_dim(probes, core * probe_half, probe_half, 1)
    probes_d = lax.dynamic_slice_in_dim(own_probes, chip * chip_cols, chip_cols, 0)
    chains_a, chains_d = [], []
    col_bits = col_count.bit_length() - 1
    quarter = probe_half // 2
    for chain in range(2):
        coef_d = probes_d[:, chain * quarter:(chain + 1) * quarter]
        for rnd in range(2):
            coef_a = doubling_sum(
                jnp.dot(chip_tile, coef_d, precision=high, preferred_element_type=jnp.float32),
                "cols", 2, col_count,
            )
            coef_d = doubling_sum(
                jnp.dot(chip_tile.T, coef_a, precision=high, preferred_element_type=jnp.float32),
                "rows", 1, row_count,
            )
        gathered = coef_a[None]
        step = 1
        while step < row_count:
            low = (row_index & step) == 0
            gathered = in_order(low, gathered, exchange(gathered, "rows", step), 0)
            step *= 2
        chains_a.append(gathered)
        gathered = coef_d.reshape((1,) * col_bits + coef_d.shape)
        for bit in range(col_bits - 1, 0, -1):
            low = (col_index >> bit) % 2 == 0
            gathered = in_order(low, gathered, exchange(gathered, "cols", 1 << bit), col_bits - 1 - bit)
        chains_d.append(gathered)
    gathered_a = jnp.concatenate(chains_a, axis=2)
    gathered_d = jnp.concatenate(chains_d, axis=-1)
    half_a = (
        gathered_a.reshape(row_count, 2, part_rows, probe_half)
        .transpose(1, 0, 2, 3)
        .reshape(snap_count, probe_half)
    )
    half_d = gathered_d.reshape(snap_count, probe_half)

    def modes(data, half):
        mine = jnp.dot(data, half, precision=fast, preferred_element_type=jnp.float32)
        theirs = jnp.dot(data, exchange(half, "cols", 1), precision=fast, preferred_element_type=jnp.float32)
        return in_order(first, mine, theirs, 1) * norm_factor

    return (modes(direct, half_d), modes(adjoint, half_a))


def solution(mesh):
    placed = (P(("rows", "cols"), None), P(("rows", "cols"), None), P())
    return jax.shard_map(
        shards,
        mesh=mesh,
        in_specs=placed,
        out_specs=(P(("rows", "cols"), None), P(("rows", "cols"), None)),
        check_vma=False,
    )
```

```python
import math

import jax
import jax.numpy as jnp
from jax import lax
from jax.sharding import PartitionSpec as P


def exchange(x, axis, step):
    count = lax.axis_size(axis)
    return lax.ppermute(x, axis, [(i, i ^ step) for i in range(count)])


def doubling_sum(x, axis, first, last):
    step = first
    while step < last:
        x = x + exchange(x, axis, step)
        step *= 2
    return x


def in_order(first, mine, theirs, axis):
    return jnp.concatenate(
        [jnp.where(first, mine, theirs), jnp.where(first, theirs, mine)], axis=axis
    )


def shards(direct, adjoint, probes):
    high = lax.Precision.HIGHEST
    fast = lax.Precision.HIGH
    row_count = lax.axis_size("rows")
    col_count = lax.axis_size("cols")
    chip_count = col_count // 2
    state_rows, snap_count = direct.shape
    probe_half = probes.shape[1] // 2
    half_rows = snap_count // 2
    part_rows = half_rows // row_count
    chip_cols = snap_count // chip_count
    scale = 1.0 / math.sqrt(state_rows * row_count * col_count * snap_count)
    norm_factor = 1.0 / math.sqrt(snap_count)
    col_index = lax.axis_index("cols")
    core = col_index % 2
    chip = col_index // 2
    first = core == 0
    row_bits = row_count.bit_length() - 1
    row_index = lax.axis_index("rows")
    chunk_cols = snap_count // row_bits

    def partial_rows(start, rot):
        columns = lax.dynamic_slice_in_dim(adjoint, start, half_rows, 1)
        snaps = direct[:, rot * chunk_cols:(rot + 1) * chunk_cols]
        return jnp.dot(columns.T, snaps, precision=fast, preferred_element_type=jnp.float32) * scale

    chunks = []
    for rot in range(row_bits):
        received = exchange(partial_rows((1 - core) * half_rows, rot), "cols", 1)
        kept_rows = lax.optimization_barrier(partial_rows(core * half_rows, rot))
        part = kept_rows + received
        part = part.reshape((2,) * row_bits + (part_rows, chunk_cols))
        left = list(range(row_bits - 1, -1, -1))
        for k in range(row_bits):
            bit = (rot + k) % row_bits
            axis = left.index(bit)
            mine = (row_index >> bit) % 2
            kept = lax.dynamic_index_in_dim(part, mine, axis=axis, keepdims=False)
            sent = lax.dynamic_index_in_dim(part, 1 - mine, axis=axis, keepdims=False)
            part = kept + exchange(sent, "rows", 1 << bit)
            left.pop(axis)
        chunks.append(part)
    strip = jnp.concatenate(chunks, axis=1)
    bits = chip_count.bit_length() - 1
    strip = strip.reshape((part_rows,) + (2,) * bits + (chip_cols,))
    for bit in range(bits):
        mine = (chip >> bit) % 2
        kept = lax.dynamic_index_in_dim(strip, mine, axis=strip.ndim - 2, keepdims=False)
        sent = lax.dynamic_index_in_dim(strip, 1 - mine, axis=strip.ndim - 2, keepdims=False)
        strip = kept + exchange(sent, "cols", 2 << bit)
    tile = strip
    chip_tile = in_order(first, tile, exchange(tile, "cols", 1), 0)
    own_probes = lax.dynamic_slice_in_dim(probes, core * probe_half, probe_half, 1)
    probes_d = lax.dynamic_slice_in_dim(own_probes, chip * chip_cols, chip_cols, 0)
    chains_a, chains_d = [], []
    col_bits = col_count.bit_length() - 1
    quarter = probe_half // 2
    for chain in range(2):
        coef_d = probes_d[:, chain * quarter:(chain + 1) * quarter]
        for rnd in range(2):
            coef_a = doubling_sum(
                jnp.dot(chip_tile, coef_d, precision=high, preferred_element_type=jnp.float32),
                "cols", 2, col_count,
            )
            coef_d = doubling_sum(
                jnp.dot(chip_tile.T, coef_a, precision=high, preferred_element_type=jnp.float32),
                "rows", 1, row_count,
            )
        gathered = coef_a[None]
        step = 1
        while step < row_count:
            low = (row_index & step) == 0
            gathered = in_order(low, gathered, exchange(gathered, "rows", step), 0)
            step *= 2
        chains_a.append(gathered)
        gathered = coef_d.reshape((1,) * col_bits + coef_d.shape)
        for bit in range(col_bits - 1, -1, -1):
            low = (col_index >> bit) % 2 == 0
            gathered = in_order(low, gathered, exchange(gathered, "cols", 1 << bit), col_bits - 1 - bit)
        chains_d.append(gathered)
    gathered_a = jnp.concatenate(chains_a, axis=2)
    gathered_d = jnp.concatenate(chains_d, axis=-1)
    half_a = (
        gathered_a.reshape(row_count, 2, part_rows, probe_half)
        .transpose(1, 0, 2, 3)
        .reshape(snap_count, probe_half)
    )
    full_a = in_order(first, half_a, exchange(half_a, "cols", 1), 1)
    full_d = (
        gathered_d.reshape(chip_count, 2, chip_cols, probe_half)
        .transpose(0, 2, 1, 3)
        .reshape(snap_count, 2 * probe_half)
    )
    direct_sum = jnp.dot(direct, full_d, precision=fast, preferred_element_type=jnp.float32)
    adjoint_sum = jnp.dot(adjoint, full_a, precision=fast, preferred_element_type=jnp.float32)
    return (direct_sum * norm_factor, adjoint_sum * norm_factor)


def solution(mesh):
    placed = (P(("rows", "cols"), None), P(("rows", "cols"), None), P())
    return jax.shard_map(
        shards,
        mesh=mesh,
        in_specs=placed,
        out_specs=(P(("rows", "cols"), None), P(("rows", "cols"), None)),
        check_vma=False,
    )
```

```python
import math

import jax
import jax.numpy as jnp
from jax import lax
from jax.sharding import PartitionSpec as P


def exchange(x, axis, step):
    count = lax.axis_size(axis)
    return lax.ppermute(x, axis, [(i, i ^ step) for i in range(count)])


def doubling_sum(x, axis, first, last):
    step = first
    while step < last:
        x = x + exchange(x, axis, step)
        step *= 2
    return x


def in_order(first, mine, theirs, axis):
    return jnp.concatenate(
        [jnp.where(first, mine, theirs), jnp.where(first, theirs, mine)], axis=axis
    )


def shards(direct, adjoint, probes):
    high = lax.Precision.HIGHEST
    fast = lax.Precision.HIGH
    row_count = lax.axis_size("rows")
    col_count = lax.axis_size("cols")
    chip_count = col_count // 2
    state_rows, snap_count = direct.shape
    probe_half = probes.shape[1] // 2
    half_rows = snap_count // 2
    part_rows = half_rows // row_count
    chip_cols = snap_count // chip_count
    scale = 1.0 / math.sqrt(state_rows * row_count * col_count * snap_count)
    norm_factor = 1.0 / math.sqrt(snap_count)
    col_index = lax.axis_index("cols")
    core = col_index % 2
    chip = col_index // 2
    first = core == 0
    def partial_rows(start):
        columns = lax.dynamic_slice_in_dim(adjoint, start, half_rows, 1)
        return jnp.dot(columns.T, direct, precision=fast, preferred_element_type=jnp.float32) * scale

    received = exchange(partial_rows((1 - core) * half_rows), "cols", 1)
    kept_rows = lax.optimization_barrier(partial_rows(core * half_rows))
    chip_sum = kept_rows + received
    row_bits = row_count.bit_length() - 1
    row_index = lax.axis_index("rows")
    chunk_cols = snap_count // row_bits
    chunks = []
    for rot in range(row_bits):
        part = chip_sum[:, rot * chunk_cols:(rot + 1) * chunk_cols]
        part = part.reshape((2,) * row_bits + (part_rows, chunk_cols))
        left = list(range(row_bits - 1, -1, -1))
        for k in range(row_bits):
            bit = (rot + k) % row_bits
            axis = left.index(bit)
            mine = (row_index >> bit) % 2
            kept = lax.dynamic_index_in_dim(part, mine, axis=axis, keepdims=False)
            sent = lax.dynamic_index_in_dim(part, 1 - mine, axis=axis, keepdims=False)
            part = kept + exchange(sent, "rows", 1 << bit)
            left.pop(axis)
        chunks.append(part)
    strip = jnp.concatenate(chunks, axis=1)
    bits = chip_count.bit_length() - 1
    strip = strip.reshape((part_rows,) + (2,) * bits + (chip_cols,))
    orders = (list(range(bits)), list(range(bits - 1, -1, -1)))
    lefts = [list(range(bits - 1, -1, -1)) for _ in orders]
    for k in range(bits):
        halves = []
        for order, left in zip(orders, lefts):
            bit = order[k]
            axis = 1 + left.index(bit)
            mine = (chip >> bit) % 2
            halves.append((
                lax.dynamic_index_in_dim(strip, mine, axis=axis, keepdims=False),
                lax.dynamic_index_in_dim(strip, 1 - mine, axis=axis, keepdims=False),
            ))
            left.remove(bit)
        kept = jnp.where(first, halves[0][0], halves[1][0])
        sent = jnp.where(first, halves[0][1], halves[1][1])
        pairs = [(i, i ^ (2 << orders[i % 2][k])) for i in range(col_count)]
        strip = kept + lax.ppermute(sent, "cols", pairs)
    tile = strip
    chip_tile = in_order(first, tile, exchange(tile, "cols", 1), 0)
    own_probes = lax.dynamic_slice_in_dim(probes, core * probe_half, probe_half, 1)
    probes_d = lax.dynamic_slice_in_dim(own_probes, chip * chip_cols, chip_cols, 0)
    chains_a, chains_d = [], []
    col_bits = col_count.bit_length() - 1
    quarter = probe_half // 2
    for chain in range(2):
        coef_d = probes_d[:, chain * quarter:(chain + 1) * quarter]
        for rnd in range(2):
            coef_a = doubling_sum(
                jnp.dot(chip_tile, coef_d, precision=high, preferred_element_type=jnp.float32),
                "cols", 2, col_count,
            )
            coef_d = doubling_sum(
                jnp.dot(chip_tile.T, coef_a, precision=high, preferred_element_type=jnp.float32),
                "rows", 1, row_count,
            )
        gathered = coef_a[None]
        step = 1
        while step < row_count:
            low = (row_index & step) == 0
            gathered = in_order(low, gathered, exchange(gathered, "rows", step), 0)
            step *= 2
        chains_a.append(gathered)
        gathered = coef_d.reshape((1,) * col_bits + coef_d.shape)
        for bit in range(col_bits - 1, -1, -1):
            low = (col_index >> bit) % 2 == 0
            gathered = in_order(low, gathered, exchange(gathered, "cols", 1 << bit), col_bits - 1 - bit)
        chains_d.append(gathered)
    gathered_a = jnp.concatenate(chains_a, axis=2)
    gathered_d = jnp.concatenate(chains_d, axis=-1)
    half_a = (
        gathered_a.reshape(row_count, 2, part_rows, probe_half)
        .transpose(1, 0, 2, 3)
        .reshape(snap_count, probe_half)
    )
    full_a = in_order(first, half_a, exchange(half_a, "cols", 1), 1)
    full_d = (
        gathered_d.reshape(chip_count, 2, chip_cols, probe_half)
        .transpose(0, 2, 1, 3)
        .reshape(snap_count, 2 * probe_half)
    )
    direct_sum = jnp.dot(direct, full_d, precision=fast, preferred_element_type=jnp.float32)
    adjoint_sum = jnp.dot(adjoint, full_a, precision=fast, preferred_element_type=jnp.float32)
    return (direct_sum * norm_factor, adjoint_sum * norm_factor)


def solution(mesh):
    placed = (P(("rows", "cols"), None), P(("rows", "cols"), None), P())
    return jax.shard_map(
        shards,
        mesh=mesh,
        in_specs=placed,
        out_specs=(P(("rows", "cols"), None), P(("rows", "cols"), None)),
        check_vma=False,
    )
```

```python
import math

import jax
import jax.numpy as jnp
from jax import lax
from jax.sharding import PartitionSpec as P


def exchange(x, axis, step):
    count = lax.axis_size(axis)
    return lax.ppermute(x, axis, [(i, i ^ step) for i in range(count)])


def doubling_sum(x, axis, first, last):
    step = first
    while step < last:
        x = x + exchange(x, axis, step)
        step *= 2
    return x


def in_order(first, mine, theirs, axis):
    return jnp.concatenate(
        [jnp.where(first, mine, theirs), jnp.where(first, theirs, mine)], axis=axis
    )


def shards(direct, adjoint, probes):
    high = lax.Precision.HIGHEST
    fast = lax.Precision.HIGH
    row_count = lax.axis_size("rows")
    col_count = lax.axis_size("cols")
    chip_count = col_count // 2
    state_rows, snap_count = direct.shape
    probe_half = probes.shape[1] // 2
    half_rows = snap_count // 2
    part_rows = half_rows // row_count
    chip_cols = snap_count // chip_count
    scale = 1.0 / math.sqrt(state_rows * row_count * col_count * snap_count)
    norm_factor = 1.0 / math.sqrt(snap_count)
    col_index = lax.axis_index("cols")
    core = col_index % 2
    chip = col_index // 2
    first = core == 0
    def partial_rows(start):
        columns = lax.dynamic_slice_in_dim(adjoint, start, half_rows, 1)
        return jnp.dot(columns.T, direct, precision=fast, preferred_element_type=jnp.float32) * scale

    received = exchange(partial_rows((1 - core) * half_rows), "cols", 1)
    kept_rows = lax.optimization_barrier(partial_rows(core * half_rows))
    row_bits = row_count.bit_length() - 1
    row_index = lax.axis_index("rows")
    chunk_cols = snap_count // row_bits
    chunks = []
    for rot in range(row_bits):
        pieces = [
            x[:, rot * chunk_cols:(rot + 1) * chunk_cols].reshape((2,) * row_bits + (part_rows, chunk_cols))
            for x in (kept_rows, received)
        ]
        left = list(range(row_bits - 1, -1, -1))
        for k in range(row_bits):
            bit = (rot + k) % row_bits
            axis = left.index(bit)
            mine = (row_index >> bit) % 2
            kept, sent = [
                sum(lax.dynamic_index_in_dim(x, side, axis=axis, keepdims=False) for x in pieces[1:])
                + lax.dynamic_index_in_dim(pieces[0], side, axis=axis, keepdims=False)
                for side in (mine, 1 - mine)
            ]
            pieces = [kept + exchange(sent, "rows", 1 << bit)]
            left.pop(axis)
        part = pieces[0]
        chunks.append(part)
    strip = jnp.concatenate(chunks, axis=1)
    bits = chip_count.bit_length() - 1
    strip = strip.reshape((part_rows,) + (2,) * bits + (chip_cols,))
    orders = (list(range(bits)), list(range(bits - 1, -1, -1)))
    lefts = [list(range(bits - 1, -1, -1)) for _ in orders]
    for k in range(bits):
        halves = []
        for order, left in zip(orders, lefts):
            bit = order[k]
            axis = 1 + left.index(bit)
            mine = (chip >> bit) % 2
            halves.append((
                lax.dynamic_index_in_dim(strip, mine, axis=axis, keepdims=False),
                lax.dynamic_index_in_dim(strip, 1 - mine, axis=axis, keepdims=False),
            ))
            left.remove(bit)
        kept = jnp.where(first, halves[0][0], halves[1][0])
        sent = jnp.where(first, halves[0][1], halves[1][1])
        pairs = [(i, i ^ (2 << orders[i % 2][k])) for i in range(col_count)]
        strip = kept + lax.ppermute(sent, "cols", pairs)
    tile = strip
    chip_tile = in_order(first, tile, exchange(tile, "cols", 1), 0)
    own_probes = lax.dynamic_slice_in_dim(probes, core * probe_half, probe_half, 1)
    probes_d = lax.dynamic_slice_in_dim(own_probes, chip * chip_cols, chip_cols, 0)
    chains_a, chains_d = [], []
    col_bits = col_count.bit_length() - 1
    quarter = probe_half // 2
    for chain in range(2):
        coef_d = probes_d[:, chain * quarter:(chain + 1) * quarter]
        for rnd in range(2):
            coef_a = doubling_sum(
                jnp.dot(chip_tile, coef_d, precision=high, preferred_element_type=jnp.float32),
                "cols", 2, col_count,
            )
            coef_d = doubling_sum(
                jnp.dot(chip_tile.T, coef_a, precision=high, preferred_element_type=jnp.float32),
                "rows", 1, row_count,
            )
        gathered = coef_a[None]
        step = 1
        while step < row_count:
            low = (row_index & step) == 0
            gathered = in_order(low, gathered, exchange(gathered, "rows", step), 0)
            step *= 2
        chains_a.append(gathered)
        gathered = coef_d.reshape((1,) * col_bits + coef_d.shape)
        for bit in range(col_bits - 1, -1, -1):
            low = (col_index >> bit) % 2 == 0
            gathered = in_order(low, gathered, exchange(gathered, "cols", 1 << bit), col_bits - 1 - bit)
        chains_d.append(gathered)
    gathered_a = jnp.concatenate(chains_a, axis=2)
    gathered_d = jnp.concatenate(chains_d, axis=-1)
    half_a = (
        gathered_a.reshape(row_count, 2, part_rows, probe_half)
        .transpose(1, 0, 2, 3)
        .reshape(snap_count, probe_half)
    )
    full_a = in_order(first, half_a, exchange(half_a, "cols", 1), 1)
    full_d = (
        gathered_d.reshape(chip_count, 2, chip_cols, probe_half)
        .transpose(0, 2, 1, 3)
        .reshape(snap_count, 2 * probe_half)
    )
    direct_sum = jnp.dot(direct, full_d, precision=fast, preferred_element_type=jnp.float32)
    adjoint_sum = jnp.dot(adjoint, full_a, precision=fast, preferred_element_type=jnp.float32)
    return (direct_sum * norm_factor, adjoint_sum * norm_factor)


def solution(mesh):
    placed = (P(("rows", "cols"), None), P(("rows", "cols"), None), P())
    return jax.shard_map(
        shards,
        mesh=mesh,
        in_specs=placed,
        out_specs=(P(("rows", "cols"), None), P(("rows", "cols"), None)),
        check_vma=False,
    )
```

```python
import math

import jax
import jax.numpy as jnp
from jax import lax
from jax.sharding import PartitionSpec as P


def exchange(x, axis, step):
    count = lax.axis_size(axis)
    return lax.ppermute(x, axis, [(i, i ^ step) for i in range(count)])


def doubling_sum(x, axis, first, last):
    step = first
    while step < last:
        x = x + exchange(x, axis, step)
        step *= 2
    return x


def in_order(first, mine, theirs, axis):
    return jnp.concatenate(
        [jnp.where(first, mine, theirs), jnp.where(first, theirs, mine)], axis=axis
    )


def shards(direct, adjoint, probes):
    high = lax.Precision.HIGHEST
    fast = lax.Precision.HIGH
    row_count = lax.axis_size("rows")
    col_count = lax.axis_size("cols")
    chip_count = col_count // 2
    state_rows, snap_count = direct.shape
    probe_half = probes.shape[1] // 2
    half_rows = snap_count // 2
    part_rows = half_rows // row_count
    chip_cols = snap_count // chip_count
    scale = 1.0 / math.sqrt(state_rows * row_count * col_count * snap_count)
    norm_factor = 1.0 / math.sqrt(snap_count)
    col_index = lax.axis_index("cols")
    core = col_index % 2
    chip = col_index // 2
    first = core == 0
    def partial_rows(start):
        columns = lax.dynamic_slice_in_dim(adjoint, start, half_rows, 1)
        return jnp.dot(columns.T, direct, precision=fast, preferred_element_type=jnp.float32) * scale

    received = exchange(partial_rows((1 - core) * half_rows), "cols", 1)
    kept_rows = lax.optimization_barrier(partial_rows(core * half_rows))
    chip_sum = kept_rows + received
    row_bits = row_count.bit_length() - 1
    row_index = lax.axis_index("rows")
    chunk_cols = snap_count // row_bits
    chunks = []
    for rot in range(row_bits):
        part = chip_sum[:, rot * chunk_cols:(rot + 1) * chunk_cols]
        part = part.reshape((2,) * row_bits + (part_rows, chunk_cols))
        left = list(range(row_bits - 1, -1, -1))
        for k in range(row_bits):
            bit = (rot + k) % row_bits
            axis = left.index(bit)
            mine = (row_index >> bit) % 2
            kept = lax.dynamic_index_in_dim(part, mine, axis=axis, keepdims=False)
            sent = lax.dynamic_index_in_dim(part, 1 - mine, axis=axis, keepdims=False)
            part = kept + exchange(sent, "rows", 1 << bit)
            left.pop(axis)
        chunks.append(part)
    strip = jnp.concatenate(chunks, axis=1)
    bits = chip_count.bit_length() - 1
    strip = strip.reshape((part_rows,) + (2,) * bits + (chip_cols,))
    orders = (list(range(bits)), list(range(bits - 1, -1, -1)))
    lefts = [list(range(bits - 1, -1, -1)) for _ in orders]
    for k in range(bits):
        halves = []
        for order, left in zip(orders, lefts):
            bit = order[k]
            axis = 1 + left.index(bit)
            mine = (chip >> bit) % 2
            halves.append((
                lax.dynamic_index_in_dim(strip, mine, axis=axis, keepdims=False),
                lax.dynamic_index_in_dim(strip, 1 - mine, axis=axis, keepdims=False),
            ))
            left.remove(bit)
        kept = jnp.where(first, halves[0][0], halves[1][0])
        sent = jnp.where(first, halves[0][1], halves[1][1])
        pairs = [(i, i ^ (2 << orders[i % 2][k])) for i in range(col_count)]
        strip = kept + lax.ppermute(sent, "cols", pairs)
    tile = strip
    chip_tile = in_order(first, tile, exchange(tile, "cols", 1), 0)
    own_probes = lax.dynamic_slice_in_dim(probes, core * probe_half, probe_half, 1)
    probes_d = lax.dynamic_slice_in_dim(own_probes, chip * chip_cols, chip_cols, 0)
    chains_a, chains_d = [], []
    col_bits = col_count.bit_length() - 1
    quarter = probe_half // 2
    for chain in range(2):
        coef_d = probes_d[:, chain * quarter:(chain + 1) * quarter]
        for rnd in range(2):
            coef_a = jnp.dot(chip_tile, coef_d, precision=high, preferred_element_type=jnp.float32)
            for k in range(bits):
                pairs = [(i, i ^ (2 << orders[i % 2][k])) for i in range(col_count)]
                coef_a = coef_a + lax.ppermute(coef_a, "cols", pairs)
            coef_d = doubling_sum(
                jnp.dot(chip_tile.T, coef_a, precision=high, preferred_element_type=jnp.float32),
                "rows", 1, row_count,
            )
        gathered = coef_a[None]
        step = 1
        while step < row_count:
            low = (row_index & step) == 0
            gathered = in_order(low, gathered, exchange(gathered, "rows", step), 0)
            step *= 2
        chains_a.append(gathered)
        gathered = coef_d.reshape((1,) * col_bits + coef_d.shape)
        for bit in range(col_bits - 1, -1, -1):
            low = (col_index >> bit) % 2 == 0
            gathered = in_order(low, gathered, exchange(gathered, "cols", 1 << bit), col_bits - 1 - bit)
        chains_d.append(gathered)
    gathered_a = jnp.concatenate(chains_a, axis=2)
    gathered_d = jnp.concatenate(chains_d, axis=-1)
    half_a = (
        gathered_a.reshape(row_count, 2, part_rows, probe_half)
        .transpose(1, 0, 2, 3)
        .reshape(snap_count, probe_half)
    )
    full_a = in_order(first, half_a, exchange(half_a, "cols", 1), 1)
    full_d = (
        gathered_d.reshape(chip_count, 2, chip_cols, probe_half)
        .transpose(0, 2, 1, 3)
        .reshape(snap_count, 2 * probe_half)
    )
    direct_sum = jnp.dot(direct, full_d, precision=fast, preferred_element_type=jnp.float32)
    adjoint_sum = jnp.dot(adjoint, full_a, precision=fast, preferred_element_type=jnp.float32)
    return (direct_sum * norm_factor, adjoint_sum * norm_factor)


def solution(mesh):
    placed = (P(("rows", "cols"), None), P(("rows", "cols"), None), P())
    return jax.shard_map(
        shards,
        mesh=mesh,
        in_specs=placed,
        out_specs=(P(("rows", "cols"), None), P(("rows", "cols"), None)),
        check_vma=False,
    )
```

```python
import math

import jax
import jax.numpy as jnp
from jax import lax
from jax.sharding import PartitionSpec as P


def exchange(x, axis, step):
    count = lax.axis_size(axis)
    return lax.ppermute(x, axis, [(i, i ^ step) for i in range(count)])


def doubling_sum(x, axis, first, last):
    step = first
    while step < last:
        x = x + exchange(x, axis, step)
        step *= 2
    return x


def in_order(first, mine, theirs, axis):
    return jnp.concatenate(
        [jnp.where(first, mine, theirs), jnp.where(first, theirs, mine)], axis=axis
    )


def shards(direct, adjoint, probes):
    high = lax.Precision.HIGHEST
    fast = lax.Precision.HIGH
    row_count = lax.axis_size("rows")
    col_count = lax.axis_size("cols")
    chip_count = col_count // 2
    state_rows, snap_count = direct.shape
    probe_half = probes.shape[1] // 2
    half_rows = snap_count // 2
    part_rows = half_rows // row_count
    chip_cols = snap_count // chip_count
    scale = 1.0 / math.sqrt(state_rows * row_count * col_count * snap_count)
    norm_factor = 1.0 / math.sqrt(snap_count)
    col_index = lax.axis_index("cols")
    core = col_index % 2
    chip = col_index // 2
    first = core == 0
    def partial_rows(start):
        columns = lax.dynamic_slice_in_dim(adjoint, start, half_rows, 1)
        return jnp.dot(columns.T, direct, precision=fast, preferred_element_type=jnp.float32) * scale

    received = exchange(partial_rows((1 - core) * half_rows), "cols", 1)
    kept_rows = lax.optimization_barrier(partial_rows(core * half_rows))
    chip_sum = kept_rows + received
    row_bits = row_count.bit_length() - 1
    row_index = lax.axis_index("rows")
    chunk_cols = snap_count // row_bits
    chunks = []
    for rot in range(row_bits):
        part = chip_sum[:, rot * chunk_cols:(rot + 1) * chunk_cols]
        part = part.reshape((2,) * row_bits + (part_rows, chunk_cols))
        left = list(range(row_bits - 1, -1, -1))
        for k in range(row_bits):
            bit = (rot + k) % row_bits
            axis = left.index(bit)
            mine = (row_index >> bit) % 2
            kept = lax.dynamic_index_in_dim(part, mine, axis=axis, keepdims=False)
            sent = lax.dynamic_index_in_dim(part, 1 - mine, axis=axis, keepdims=False)
            part = kept + exchange(sent, "rows", 1 << bit)
            left.pop(axis)
        chunks.append(part)
    strip = jnp.concatenate(chunks, axis=1)
    bits = chip_count.bit_length() - 1
    strip = strip.reshape((part_rows,) + (2,) * bits + (chip_cols,))
    orders = (list(range(bits)), list(range(bits - 1, -1, -1)))
    lefts = [list(range(bits - 1, -1, -1)) for _ in orders]
    for k in range(bits):
        halves = []
        for order, left in zip(orders, lefts):
            bit = order[k]
            axis = 1 + left.index(bit)
            mine = (chip >> bit) % 2
            halves.append((
                lax.dynamic_index_in_dim(strip, mine, axis=axis, keepdims=False),
                lax.dynamic_index_in_dim(strip, 1 - mine, axis=axis, keepdims=False),
            ))
            left.remove(bit)
        kept = jnp.where(first, halves[0][0], halves[1][0])
        sent = jnp.where(first, halves[0][1], halves[1][1])
        pairs = [(i, i ^ (2 << orders[i % 2][k])) for i in range(col_count)]
        strip = kept + lax.ppermute(sent, "cols", pairs)
    tile = strip
    chip_tile = in_order(first, tile, exchange(tile, "cols", 1), 0)
    own_probes = lax.dynamic_slice_in_dim(probes, core * probe_half, probe_half, 1)
    probes_d = lax.dynamic_slice_in_dim(own_probes, chip * chip_cols, chip_cols, 0)
    chains_a, chains_d = [], []
    col_bits = col_count.bit_length() - 1
    quarter = probe_half // 2
    for chain in range(2):
        coef_d = probes_d[:, chain * quarter:(chain + 1) * quarter]
        for rnd in range(2):
            coef_a = jnp.dot(chip_tile, coef_d, precision=high, preferred_element_type=jnp.float32)
            for k in range(bits):
                pairs = [(i, i ^ (2 << orders[i % 2][k])) for i in range(col_count)]
                coef_a = coef_a + lax.ppermute(coef_a, "cols", pairs)
            coef_d = jnp.dot(chip_tile.T, coef_a, precision=high, preferred_element_type=jnp.float32)
            for k in range(row_bits):
                pairs = []
                for i in range(row_count * col_count):
                    r, c = divmod(i, col_count)
                    bit = row_bits - 1 - k if c % 2 else k
                    pairs.append((i, (r ^ (1 << bit)) * col_count + c))
                coef_d = coef_d + lax.ppermute(coef_d, ("rows", "cols"), pairs)
        gathered = coef_a[None]
        step = 1
        while step < row_count:
            low = (row_index & step) == 0
            gathered = in_order(low, gathered, exchange(gathered, "rows", step), 0)
            step *= 2
        chains_a.append(gathered)
        gathered = coef_d.reshape((1,) * col_bits + coef_d.shape)
        for bit in range(col_bits - 1, -1, -1):
            low = (col_index >> bit) % 2 == 0
            gathered = in_order(low, gathered, exchange(gathered, "cols", 1 << bit), col_bits - 1 - bit)
        chains_d.append(gathered)
    gathered_a = jnp.concatenate(chains_a, axis=2)
    gathered_d = jnp.concatenate(chains_d, axis=-1)
    half_a = (
        gathered_a.reshape(row_count, 2, part_rows, probe_half)
        .transpose(1, 0, 2, 3)
        .reshape(snap_count, probe_half)
    )
    full_a = in_order(first, half_a, exchange(half_a, "cols", 1), 1)
    full_d = (
        gathered_d.reshape(chip_count, 2, chip_cols, probe_half)
        .transpose(0, 2, 1, 3)
        .reshape(snap_count, 2 * probe_half)
    )
    direct_sum = jnp.dot(direct, full_d, precision=fast, preferred_element_type=jnp.float32)
    adjoint_sum = jnp.dot(adjoint, full_a, precision=fast, preferred_element_type=jnp.float32)
    return (direct_sum * norm_factor, adjoint_sum * norm_factor)


def solution(mesh):
    placed = (P(("rows", "cols"), None), P(("rows", "cols"), None), P())
    return jax.shard_map(
        shards,
        mesh=mesh,
        in_specs=placed,
        out_specs=(P(("rows", "cols"), None), P(("rows", "cols"), None)),
        check_vma=False,
    )
```

```python
import math

import jax
import jax.numpy as jnp
from jax import lax
from jax.sharding import PartitionSpec as P


def exchange(x, axis, step):
    count = lax.axis_size(axis)
    return lax.ppermute(x, axis, [(i, i ^ step) for i in range(count)])


def doubling_sum(x, axis, first, last):
    step = first
    while step < last:
        x = x + exchange(x, axis, step)
        step *= 2
    return x


def in_order(first, mine, theirs, axis):
    return jnp.concatenate(
        [jnp.where(first, mine, theirs), jnp.where(first, theirs, mine)], axis=axis
    )


def shards(direct, adjoint, probes):
    high = lax.Precision.HIGHEST
    fast = lax.Precision.HIGH
    row_count = lax.axis_size("rows")
    col_count = lax.axis_size("cols")
    chip_count = col_count // 2
    state_rows, snap_count = direct.shape
    probe_half = probes.shape[1] // 2
    half_rows = snap_count // 2
    part_rows = half_rows // row_count
    chip_cols = snap_count // chip_count
    scale = 1.0 / math.sqrt(state_rows * row_count * col_count * snap_count)
    norm_factor = 1.0 / math.sqrt(snap_count)
    col_index = lax.axis_index("cols")
    core = col_index % 2
    chip = col_index // 2
    first = core == 0
    def partial_rows(start):
        columns = lax.dynamic_slice_in_dim(adjoint, start, half_rows, 1)
        return jnp.dot(columns.T, direct, precision=fast, preferred_element_type=jnp.float32) * scale

    received = exchange(partial_rows((1 - core) * half_rows), "cols", 1)
    kept_rows = lax.optimization_barrier(partial_rows(core * half_rows))
    chip_sum = kept_rows + received
    row_bits = row_count.bit_length() - 1
    row_index = lax.axis_index("rows")
    chunk_cols = snap_count // row_bits
    chunks = []
    for rot in range(row_bits):
        part = chip_sum[:, rot * chunk_cols:(rot + 1) * chunk_cols]
        part = part.reshape((2,) * row_bits + (part_rows, chunk_cols))
        left = list(range(row_bits - 1, -1, -1))
        for k in range(row_bits):
            bit = (rot + k) % row_bits
            axis = left.index(bit)
            mine = (row_index >> bit) % 2
            kept = lax.dynamic_index_in_dim(part, mine, axis=axis, keepdims=False)
            sent = lax.dynamic_index_in_dim(part, 1 - mine, axis=axis, keepdims=False)
            part = kept + exchange(sent, "rows", 1 << bit)
            left.pop(axis)
        chunks.append(part)
    strip = jnp.concatenate(chunks, axis=1)
    bits = chip_count.bit_length() - 1
    strip = strip.reshape((part_rows,) + (2,) * bits + (chip_cols,))
    orders = (list(range(bits)), list(range(bits - 1, -1, -1)))
    lefts = [list(range(bits - 1, -1, -1)) for _ in orders]
    for k in range(bits):
        halves = []
        for order, left in zip(orders, lefts):
            bit = order[k]
            axis = 1 + left.index(bit)
            mine = (chip >> bit) % 2
            halves.append((
                lax.dynamic_index_in_dim(strip, mine, axis=axis, keepdims=False),
                lax.dynamic_index_in_dim(strip, 1 - mine, axis=axis, keepdims=False),
            ))
            left.remove(bit)
        kept = jnp.where(first, halves[0][0], halves[1][0])
        sent = jnp.where(first, halves[0][1], halves[1][1])
        pairs = [(i, i ^ (2 << orders[i % 2][k])) for i in range(col_count)]
        strip = kept + lax.ppermute(sent, "cols", pairs)
    tile = strip
    chip_tile = in_order(first, tile, exchange(tile, "cols", 1), 0)
    own_probes = lax.dynamic_slice_in_dim(probes, core * probe_half, probe_half, 1)
    probes_d = lax.dynamic_slice_in_dim(own_probes, chip * chip_cols, chip_cols, 0)
    chains_a, chains_d = [], []
    col_bits = col_count.bit_length() - 1
    quarter = probe_half // 2
    for chain in range(2):
        coef_d = probes_d[:, chain * quarter:(chain + 1) * quarter]
        for rnd in range(2):
            coef_a = jnp.dot(chip_tile, coef_d, precision=high, preferred_element_type=jnp.float32)
            for k in range(bits):
                pairs = [(i, i ^ (2 << orders[i % 2][k])) for i in range(col_count)]
                coef_a = coef_a + lax.ppermute(coef_a, "cols", pairs)
            coef_d = doubling_sum(
                jnp.dot(chip_tile.T, coef_a, precision=high, preferred_element_type=jnp.float32),
                "rows", 1, row_count,
            )
        gathered = coef_a[None]
        for k in range(row_bits):
            pairs = []
            for i in range(row_count * col_count):
                r, c = divmod(i, col_count)
                pairs.append((i, (r ^ (1 << (row_bits - 1 - k if c % 2 else k))) * col_count + c))
            bit = jnp.where(first, k, row_bits - 1 - k)
            low = (row_index >> bit) % 2 == 0
            gathered = in_order(low, gathered, lax.ppermute(gathered, ("rows", "cols"), pairs), 0)
        rest = gathered.shape[1:]
        swapped = (
            gathered.reshape((2,) * row_bits + rest)
            .transpose(tuple(range(row_bits - 1, -1, -1)) + tuple(range(row_bits, row_bits + len(rest))))
            .reshape(gathered.shape)
        )
        chains_a.append(jnp.where(first, gathered, swapped))
        gathered = coef_d.reshape((1,) * col_bits + coef_d.shape)
        for bit in range(col_bits - 1, -1, -1):
            low = (col_index >> bit) % 2 == 0
            gathered = in_order(low, gathered, exchange(gathered, "cols", 1 << bit), col_bits - 1 - bit)
        chains_d.append(gathered)
    gathered_a = jnp.concatenate(chains_a, axis=2)
    gathered_d = jnp.concatenate(chains_d, axis=-1)
    half_a = (
        gathered_a.reshape(row_count, 2, part_rows, probe_half)
        .transpose(1, 0, 2, 3)
        .reshape(snap_count, probe_half)
    )
    full_a = in_order(first, half_a, exchange(half_a, "cols", 1), 1)
    full_d = (
        gathered_d.reshape(chip_count, 2, chip_cols, probe_half)
        .transpose(0, 2, 1, 3)
        .reshape(snap_count, 2 * probe_half)
    )
    direct_sum = jnp.dot(direct, full_d, precision=fast, preferred_element_type=jnp.float32)
    adjoint_sum = jnp.dot(adjoint, full_a, precision=fast, preferred_element_type=jnp.float32)
    return (direct_sum * norm_factor, adjoint_sum * norm_factor)


def solution(mesh):
    placed = (P(("rows", "cols"), None), P(("rows", "cols"), None), P())
    return jax.shard_map(
        shards,
        mesh=mesh,
        in_specs=placed,
        out_specs=(P(("rows", "cols"), None), P(("rows", "cols"), None)),
        check_vma=False,
    )
```
